128 devices in a mesh: sec: 2 (over core), tile: 64 (over y, x, z).
Axes of the slice: x: 4, y: 4, z: 4, core: 2. Of those that a mesh axis runs over, the one named last changes fastest.
Arguments:
- land_wind: float32 [16384, 128], P(('sec', 'tile')), may hold values from 0.15 to 0.9
- land_moist: float32 [16384, 128], P(('sec', 'tile')), may hold values from 0 to 0.3
- texture: int32 [16384, 128], P(('sec', 'tile')), may hold values from 0 to 3
- land_index: int32 [16384, 128], P(('sec', 'tile')), may hold values from 0 to 32767
- erod_map: float32 [4194304], P(('sec', 'tile')), may hold values from 0.2 to 1
- mass_frac: float32 [4, 12], replicated, may hold values from 0.02 to 0.3
- blast_table: float32 [4, 8, 12], replicated, may hold values from 0.05 to 1
- dest_tile: int32 [16384, 1], P(('sec', 'tile')), may hold values from 0 to 127; in each aligned block of 128 rows (0 to 127, 128 to 255, ...) at most 2 rows name the same one
- regrid_w: bfloat16 [16384, 128, 256], P(('sec', 'tile')), may hold values from 0 to 0.25, as said below
- atm_state: float32 [3, 16, 32768], P(None, None, ('sec', 'tile')), may hold values from -5 to 5
- dust_mix: float32 [8, 16, 32768], P(None, None, ('sec', 'tile')), may hold values from 0 to 1
- mixing: float32 [15, 32768], P(None, ('sec', 'tile')), may hold values from 0.1 to 10
- settle: float32 [8], replicated, may hold values from 0.05 to 0.5
Outputs:
- land_fields: float32 [2, 16384, 128], P(None, ('sec', 'tile'))
- dust_out: float32 [8, 16, 32768], P(None, None, ('sec', 'tile'))
The draws below stay inside these ranges and needn't reach their ends.
Inputs may be any that keep to these rules, and one draw needn't show every extreme that they name: `land_index`: each land cell's index points into its own device's 32768 cells of erod_map. `dest_tile`: among the 128 blocks of one device at most 2 name the same tile, a bound that some block reaches. `regrid_w`: each land cell has 1 to 4 positive weights, of 0.05 or more, on adjacent columns of its tile, and 0 elsewhere.
All inputs are finite; a program needn't handle non-finite values.
Results may differ from the reference program's by a relative error of at most 0.0023.
Values may be sent and summed in bfloat16 or wider, within the bound.
No kernel may reach another device: no remote copies, remote signals or barrier semaphores. Data moves between devices by JAX's collectives and lax.ppermute only.
A program may use at most 64 MiB of HBM per device.

```python
import math
import jax
import jax.numpy as jnp
import numpy as np
from jax import lax

BINS = 12
DBINS = 8
TEXTURES = 4
BL = 128
LEV = 16
NBLK_DEV = 128
AC = 256
CAP = 2
NB = 16384
COLS = 32768
GRID_DEV = 32768
GRID = 4194304
DEVICES = 128


def draw_regrid_w(key, part):
    key_jitter = jax.random.fold_in(key, 11)
    key_count = jax.random.fold_in(key, 12)
    key_value = jax.random.fold_in(key, 13)
    cells = jnp.arange(BL).astype(jnp.int32)
    base = cells * (AC - 4) // BL
    jitter = jax.random.randint(key_jitter, (NB, BL), 0, 2).astype(jnp.int32)
    first = jnp.minimum(base[None, :] + jitter, AC - 4)
    count = jax.random.randint(key_count, (NB, BL), 1, 5).astype(jnp.int32)
    column = jnp.arange(AC).astype(jnp.int32)
    inside = (column[None, None, :] >= first[:, :, None]) & (column[None, None, :] < first[:, :, None] + count[:, :, None])
    values = jax.random.uniform(key_value, (NB, BL, AC), jnp.float32, 0.1, 0.25)
    return jnp.where(inside, values, jnp.float32(0.0)).astype(jnp.bfloat16)


def set_ends(values, rng, least, largest):
    longest = values.shape.index(max(values.shape))
    spots = []
    for shift in (0, 1):
        where = [jax.random.randint(jax.random.fold_in(rng, axis), (), 0, length) for axis, length in enumerate(values.shape)]
        where[longest] = (where[longest] + shift) % values.shape[longest]
        spots.append(tuple(where))
    return values.at[spots[0]].set(least).at[spots[1]].set(largest)


def shard_levels(own_key, shape, split, smallest, top_value):
    def one(axis_at, parts):
        draws = jax.random.uniform(jax.random.fold_in(jax.random.fold_in(own_key, 6), axis_at), (parts,), jnp.float32, smallest / len(split), top_value / len(split))
        return jnp.repeat(jnp.exp(draws), shape[axis_at] // parts).reshape((-1,) + (1,) * (len(shape) - axis_at - 1))

    loudness = one(*split[0])
    for cut in split[1:]:
        loudness = loudness * one(*cut)
    return loudness


def assign_block(key, own, number, rows, amount, top, reach, lean):
    sequence = jax.random.permutation(key, amount)
    heavy_load, common = portions_of(amount, rows * top, reach, lean, True), portions_of(amount, rows * top, reach, lean, False)
    places = jnp.arange(amount)

    def named(tallies, turn):
        used = int((tallies > 0).sum())
        fixed = max(1, used // 4)
        shifted = fixed + (places - fixed + turn * (used - fixed)) % max(1, amount - fixed)
        return jnp.zeros((amount,), jnp.int32).at[sequence[jnp.where(places < fixed, places, shifted)]].set(jnp.asarray(tallies, jnp.int32))

    tallies = jnp.where(number % 4 == 0, named(heavy_load, number // 4), named(common, number - number // 4 - 1))
    mixed = jax.random.permutation(jax.random.fold_in(own, 3), amount)
    donor, receiver = mixed[0:amount // 2 * 2:2], mixed[1:amount // 2 * 2:2]
    margin = jnp.minimum(tallies[donor] - 1, reach - tallies[receiver]) // 2
    margin = jnp.where((donor == sequence[0]) | (receiver == sequence[0]) | (tallies[receiver] == 0), 0, jnp.maximum(margin, 0))
    shifted = jax.random.randint(jax.random.fold_in(own, 4), (amount // 2,), 0, 1 << 20) % (margin + 1)
    tallies = tallies.at[donor].add(-shifted).at[receiver].add(shifted)
    items = jnp.searchsorted(jnp.cumsum(tallies), jnp.arange(rows * top), side="right").astype(jnp.int32)
    grid = items.reshape(top, rows).T
    grid = grid[jax.random.permutation(jax.random.fold_in(own, 1), rows)]
    turn = jax.random.randint(jax.random.fold_in(own, 2), (rows, 1), 0, top)
    return jnp.take_along_axis(grid, (jnp.arange(top)[None, :] + turn) % top, axis=1)


def portions_of(amount, total, reach, lean, full):
    weights = [(1 << 20) // math.isqrt(rank ** lean) + 1 for rank in range(1, amount + 1)]
    largest = reach if full else min(reach, max(-(-total // amount), total * weights[0] // sum(weights)))
    least = 1 if total - largest >= amount - 1 else 0
    counts, surplus = [largest] + [least] * (amount - 1), total - largest - least * (amount - 1)
    while surplus > 0:
        movable = [i for i in range(1, amount) if counts[i] < largest] or [i for i in range(1, amount) if counts[i] < reach]
        mass, left = sum([weights[i] for i in movable]), surplus
        for i in movable:
            more = min(reach - counts[i], max(1, left * weights[i] // mass), surplus)
            counts[i] = counts[i] + more
            surplus = surplus - more
    return np.array(counts)


def centred(key, shape, width, most, pieces=(), held_as=jnp.bfloat16):
    entries = width * jax.random.normal(key, shape, jnp.float32)
    if pieces:
        entries = entries * shard_levels(key, shape, pieces, -0.22, 0.18)
    return jnp.clip(entries, -most, most).astype(held_as)


def setup_inputs(seed: int = 0) -> dict:
    key_of = jax.random.split(jax.random.key(seed), 14)
    land_wind = jnp.clip(jnp.exp(math.log(0.9) - 1.7917594 * jax.random.uniform(key_of[0], (NB, BL), jnp.float32) ** shard_levels(key_of[0], (NB, BL), ((0, 128),), -0.2, 0.2)), 0.15, 0.9)
    land_moist = jnp.clip(0.3 * jax.random.uniform(key_of[1], (NB, BL), jnp.float32) ** shard_levels(key_of[1], (NB, BL), ((0, 128),), -0.2, 0.2), 0.0, 0.3)
    texture = set_ends(jax.random.randint(key_of[2], (NB, BL), 0, TEXTURES), jax.random.fold_in(key_of[2], 1), 0, TEXTURES - 1).astype(jnp.int32)
    land_index = set_ends(jax.random.randint(key_of[3], (NB, BL), 0, GRID_DEV), jax.random.fold_in(key_of[3], 1), 0, GRID_DEV - 1).astype(jnp.int32)
    erod_map = jnp.clip(0.2 + 0.8 * jax.random.uniform(key_of[4], (GRID,), jnp.float32) ** shard_levels(key_of[4], (GRID,), ((0, 128),), -0.2, 0.2), 0.2, 1.0)
    mass_frac = jnp.clip(jnp.exp(jax.random.uniform(key_of[5], (TEXTURES, BINS), jnp.float32, math.log(0.02), math.log(0.3))), 0.02, 0.3)
    blast_table = jnp.clip(jnp.exp(jax.random.uniform(key_of[6], (TEXTURES, DBINS, BINS), jnp.float32, math.log(0.05), math.log(1.0))), 0.05, 1.0)
    dest_tile_keys = jax.random.split(jax.random.fold_in(key_of[7], 1), NB // NBLK_DEV)
    dest_tile_turns = jax.random.permutation(jax.random.fold_in(key_of[7], 3), NB // NBLK_DEV)
    dest_tile = jax.vmap(lambda own, number: assign_block(jax.random.fold_in(key_of[7], 2), own, number, NBLK_DEV, DEVICES, 1, CAP, 2))(dest_tile_keys, dest_tile_turns).reshape((NB, 1))
    regrid_w = draw_regrid_w(jax.random.fold_in(key_of[13], 71), 0)
    atm_state = centred(key_of[9], (3, LEV, COLS), 1.0, 5.0, ((2, 128),), jnp.float32)
    dust_mix = jnp.clip(1.0 * jax.random.uniform(key_of[10], (DBINS, LEV, COLS), jnp.float32) ** shard_levels(key_of[10], (DBINS, LEV, COLS), ((2, 128),), -0.2, 0.2), 0.0, 1.0)
    mixing = jnp.clip(jnp.exp(math.log(10.0) - 4.6051702 * jax.random.uniform(key_of[11], (LEV - 1, COLS), jnp.float32) ** shard_levels(key_of[11], (LEV - 1, COLS), ((1, 128),), -0.2, 0.2)), 0.1, 10.0)
    settle = jnp.clip(jax.random.uniform(key_of[12], (DBINS,), jnp.float32, 0.05, 0.5), 0.05, 0.5)
    return {"land_wind": land_wind, "land_moist": land_moist, "texture": texture, "land_index": land_index, "erod_map": erod_map, "mass_frac": mass_frac, "blast_table": blast_table, "dest_tile": dest_tile, "regrid_w": regrid_w, "atm_state": atm_state, "dust_mix": dust_mix, "mixing": mixing, "settle": settle}


def threshold_table(count):
    diameter = 4e-05 * jnp.power(jnp.float32(1.35), jnp.arange(count).astype(jnp.float32))
    return jnp.sqrt(0.0123 * (2160.0 * 9.81 * diameter + 0.0003 / (1.227 * diameter)))

def emit(wind_rows, moist_rows, texture_rows, erodible, mass_frac, blast_table, base_thresh):
    high = lax.Precision.HIGHEST
    thresh = base_thresh[:, None, None] * jnp.sqrt(1.0 + 12.1 * moist_rows)[None]
    classes = jnp.arange(mass_frac.shape[0]).astype(jnp.int32)
    onehot = (texture_rows[None] == classes[:, None, None]).astype(jnp.float32)
    fraction = jnp.einsum('tb,tnl->bnl', mass_frac, onehot, precision=high)
    speed = wind_rows[None]
    salt = 40.0 * fraction * erodible[None] * (speed + thresh) * jnp.maximum(speed * speed - thresh * thresh, 0.0)
    blasted = jnp.einsum('tkb,bnl->tknl', blast_table, salt, precision=high)
    emission = lax.optimization_barrier(jnp.sum(blasted * onehot[:, None], axis=0))
    return jnp.transpose(emission, (1, 0, 2)).astype(jnp.bfloat16)

def solve(right_side, coupling, sinking):
    levels = right_side.shape[1]
    sink_col = sinking[:, None]
    zero_row = jnp.zeros_like(coupling[0])
    ratios = []
    partial_value = []
    ratio_prev = None
    part_prev = None
    for level in range(levels):
        lower_c = coupling[level - 1] if level > 0 else zero_row
        upper_c = coupling[level] if level < levels - 1 else zero_row
        diagonal = 1.0 + lower_c[None] + upper_c[None] + sink_col
        if level == 0:
            pivot = diagonal
            part_now = right_side[:, level] / pivot
        else:
            pivot = diagonal + lower_c[None] * ratio_prev
            part_now = (right_side[:, level] + lower_c[None] * part_prev) / pivot
        if level < levels - 1:
            ratio_now = -(upper_c[None] + sink_col) / pivot
        else:
            ratio_now = jnp.zeros_like(pivot)
        ratios.append(ratio_now)
        partial_value.append(part_now)
        ratio_prev = ratio_now
        part_prev = part_now
    result = [None] * levels
    result[levels - 1] = partial_value[levels - 1]
    for level in range(levels - 2, -1, -1):
        result[level] = partial_value[level] - ratios[level] * result[level + 1]
    return jnp.stack(result, axis=1)

def reference(land_wind, land_moist, texture, land_index, erod_map, mass_frac, blast_table, dest_tile, regrid_w, atm_state, dust_mix, mixing, settle):
    high = lax.Precision.HIGHEST
    base_thresh = threshold_table(mass_frac.shape[1])
    items = (land_wind.reshape(DEVICES, NBLK_DEV, BL), land_moist.reshape(DEVICES, NBLK_DEV, BL), texture.reshape(DEVICES, NBLK_DEV, BL), land_index.reshape(DEVICES, NBLK_DEV, BL), erod_map.reshape(DEVICES, GRID_DEV), dest_tile.reshape(DEVICES, NBLK_DEV), regrid_w.reshape(DEVICES, NBLK_DEV, BL, AC))

    def forward(total, item):
        wind_rows, moist_rows, texture_rows, index_rows, soil_map, targets, weights = item
        erodible = soil_map[index_rows]
        emission = emit(wind_rows, moist_rows, texture_rows, erodible, mass_frac, blast_table, base_thresh)
        partial_flux = jnp.einsum('gkl,gla->gka', emission.astype(jnp.float32), weights.astype(jnp.float32), precision=high)
        return (total + jax.ops.segment_sum(partial_flux, targets, num_segments=DEVICES), None)
    start = jnp.zeros((DEVICES, DBINS, AC), jnp.float32)
    summed, _ = lax.scan(forward, start, items)
    flux = jnp.transpose(summed * (float(AC) / float(BL * NBLK_DEV)), (1, 0, 2)).reshape(DBINS, COLS)
    state = solve(atm_state, mixing, jnp.zeros((3,), jnp.float32))
    speed = jnp.sqrt(state[0, 0] ** 2 + state[1, 0] ** 2 + 0.25)
    surface = jnp.stack([speed, state[2, 0]]).astype(jnp.bfloat16)
    by_tile = jnp.transpose(surface.reshape(2, DEVICES, AC), (1, 0, 2))

    def backward(item):
        moist_rows, targets, weights = item
        picked = by_tile[targets]
        weights_wide = weights.astype(jnp.float32)
        numer = jnp.einsum('gla,gka->kgl', weights_wide, picked.astype(jnp.float32), precision=high)
        denom = lax.optimization_barrier(jnp.sum(weights_wide, axis=2))
        return jnp.stack([numer[0] / denom, 0.5 * moist_rows + 0.5 * numer[1] / denom])
    back = lax.map(backward, (items[1], items[5], items[6]))
    land_fields = jnp.transpose(back, (1, 0, 2, 3)).reshape(2, NB, BL)
    loaded = dust_mix.at[:, 0, :].add(flux)
    dust_out = solve(loaded, mixing, settle)
    return (land_fields, dust_out)
```

```python
import jax
import jax.numpy as jnp
from jax import lax
from jax.sharding import PartitionSpec as P


def threshold_table(count):
    diameter = 4e-05 * jnp.power(jnp.float32(1.35), jnp.arange(count).astype(jnp.float32))
    return jnp.sqrt(0.0123 * (2160.0 * 9.81 * diameter + 0.0003 / (1.227 * diameter)))


def emit(wind_rows, moist_rows, texture_rows, erodible, mass_frac, blast_table, base_thresh):
    high = lax.Precision.HIGHEST
    thresh = base_thresh[:, None, None] * jnp.sqrt(1.0 + 12.1 * moist_rows)[None]
    classes = jnp.arange(mass_frac.shape[0])
    onehot = (texture_rows[None] == classes[:, None, None]).astype(jnp.float32)
    fraction = jnp.einsum("tb,tnl->bnl", mass_frac, onehot, precision=high)
    speed = wind_rows[None]
    salt = (
        40.0
        * fraction
        * erodible[None]
        * (speed + thresh)
        * jnp.maximum(speed * speed - thresh * thresh, 0.0)
    )
    blasted = jnp.einsum("tkb,bnl->tknl", blast_table, salt, precision=high)
    emission = jnp.sum(blasted * onehot[:, None], axis=0)
    return jnp.transpose(emission, (1, 0, 2)).astype(jnp.bfloat16)


def solve(right_side, coupling, sinking):
    levels = right_side.shape[1]
    sink_col = sinking[:, None]
    zero_row = jnp.zeros_like(coupling[0])
    ratios = []
    partial_value = []
    ratio_prev = None
    part_prev = None
    for level in range(levels):
        lower_c = coupling[level - 1] if level > 0 else zero_row
        upper_c = coupling[level] if level < levels - 1 else zero_row
        diagonal = 1.0 + lower_c[None] + upper_c[None] + sink_col
        if level == 0:
            pivot = diagonal
            part_now = right_side[:, level] / pivot
        else:
            pivot = diagonal + lower_c[None] * ratio_prev
            part_now = (right_side[:, level] + lower_c[None] * part_prev) / pivot
        if level < levels - 1:
            ratio_now = -(upper_c[None] + sink_col) / pivot
        else:
            ratio_now = jnp.zeros_like(pivot)
        ratios.append(ratio_now)
        partial_value.append(part_now)
        ratio_prev = ratio_now
        part_prev = part_now
    result = [None] * levels
    result[levels - 1] = partial_value[levels - 1]
    for level in range(levels - 2, -1, -1):
        result[level] = partial_value[level] - ratios[level] * result[level + 1]
    return jnp.stack(result, axis=1)


def on_device(
    land_wind,
    land_moist,
    texture,
    land_index,
    erod_map,
    mass_frac,
    blast_table,
    dest_tile,
    regrid_w,
    atm_state,
    dust_mix,
    mixing,
    settle,
):
    high = lax.Precision.HIGHEST
    nblocks, ncells = land_wind.shape
    columns = atm_state.shape[2]
    nbins = blast_table.shape[1]
    devices = lax.axis_size(("sec", "tile"))
    state = solve(atm_state, mixing, jnp.zeros((3,), jnp.float32))
    speed = jnp.sqrt(state[0, 0] ** 2 + state[1, 0] ** 2 + 0.25)
    surface = jnp.stack([speed, state[2, 0]]).astype(jnp.bfloat16).reshape(1, 2 * columns)
    spread = jnp.broadcast_to(surface, (devices, 2 * columns))
    gathered = lax.all_to_all(spread, ("sec", "tile"), split_axis=0, concat_axis=0, tiled=True)
    base_thresh = threshold_table(mass_frac.shape[1])
    erodible = erod_map[land_index]
    emission = emit(land_wind, land_moist, texture, erodible, mass_frac, blast_table, base_thresh)
    partial_flux = jnp.einsum(
        "gkl,gla->gka", emission, regrid_w, preferred_element_type=jnp.float32
    )
    flat_flux = partial_flux.reshape(nblocks, nbins * columns)
    targets = dest_tile[:, 0]
    onehot = (targets[:, None] == jnp.arange(devices)[None, :]).astype(jnp.float32)
    capacity = max(2, 2 * nblocks // devices)
    before = jnp.cumsum(onehot, axis=0) - onehot
    ranking = jnp.sum(before * onehot, axis=1).astype(jnp.int32)
    slot_of = targets * capacity + ranking
    placing = (jnp.arange(devices * capacity)[:, None] == slot_of[None, :]).astype(jnp.float32)
    outgoing = jnp.dot(placing, flat_flux, precision=high).reshape(
        devices, capacity * nbins * columns
    )
    incoming = lax.all_to_all(
        outgoing.astype(jnp.bfloat16), ("sec", "tile"), split_axis=0, concat_axis=0, tiled=True
    ).astype(outgoing.dtype)
    flux = jnp.sum(incoming.reshape(devices * capacity, nbins, columns), axis=0)
    flux = flux * (float(columns) / float(ncells * nblocks))
    loaded = dust_mix.at[:, 0, :].add(flux)
    dust_out = solve(loaded, mixing, settle)
    picked = jnp.dot(onehot.astype(jnp.bfloat16), gathered, preferred_element_type=jnp.float32)
    picked = picked.astype(jnp.bfloat16).reshape(nblocks, 2, columns)
    numer = jnp.einsum("gla,gka->kgl", regrid_w, picked, preferred_element_type=jnp.float32)
    denom = jnp.sum(regrid_w, axis=2, dtype=jnp.float32)
    land_fields = jnp.stack([numer[0] / denom, 0.5 * land_moist + 0.5 * numer[1] / denom])
    return (land_fields, dust_out)


def solution(mesh):
    in_specs = (
        P(("sec", "tile"), None),
        P(("sec", "tile"), None),
        P(("sec", "tile"), None),
        P(("sec", "tile"), None),
        P(("sec", "tile")),
        P(),
        P(),
        P(("sec", "tile"), None),
        P(("sec", "tile"), None, None),
        P(None, None, ("sec", "tile")),
        P(None, None, ("sec", "tile")),
        P(None, ("sec", "tile")),
        P(),
    )
    out_specs = (P(None, ("sec", "tile"), None), P(None, None, ("sec", "tile")))
    return jax.shard_map(
        on_device, mesh=mesh, in_specs=in_specs, out_specs=out_specs, check_vma=False
    )
```

```python
import jax
import jax.numpy as jnp
from jax import lax
from jax.sharding import PartitionSpec as P


def threshold_table(count):
    diameter = 4e-05 * jnp.power(jnp.float32(1.35), jnp.arange(count).astype(jnp.float32))
    return jnp.sqrt(0.0123 * (2160.0 * 9.81 * diameter + 0.0003 / (1.227 * diameter)))


def emit(wind_rows, moist_rows, texture_rows, erodible, mass_frac, blast_table, base_thresh):
    high = lax.Precision.HIGHEST
    thresh = base_thresh[:, None, None] * jnp.sqrt(1.0 + 12.1 * moist_rows)[None]
    classes = jnp.arange(mass_frac.shape[0])
    onehot = (texture_rows[None] == classes[:, None, None]).astype(jnp.float32)
    fraction = jnp.einsum("tb,tnl->bnl", mass_frac, onehot, precision=high)
    speed = wind_rows[None]
    salt = (
        40.0
        * fraction
        * erodible[None]
        * (speed + thresh)
        * jnp.maximum(speed * speed - thresh * thresh, 0.0)
    )
    blasted = jnp.einsum("tkb,bnl->tknl", blast_table, salt, precision=high)
    emission = jnp.sum(blasted * onehot[:, None], axis=0)
    return jnp.transpose(emission, (1, 0, 2)).astype(jnp.bfloat16)


def lookup(table, index):
    rows = table.shape[0] // 128
    flat = index.reshape(-1)
    high_part = flat // 128
    low_part = flat % 128
    pick_row = (lax.broadcasted_iota(jnp.int32, (rows, flat.shape[0]), 0) == high_part[None, :]).astype(jnp.bfloat16)
    grid = table.reshape(rows, 128)
    first = grid.astype(jnp.bfloat16)
    rest = grid - first.astype(jnp.float32)
    second = rest.astype(jnp.bfloat16)
    third = (rest - second.astype(jnp.float32)).astype(jnp.bfloat16)
    dims = (((0,), (0,)), ((), ()))
    parts = [lax.dot_general(p, pick_row, dims, preferred_element_type=jnp.float32) for p in (first, second, third)]
    row_values = (parts[0] + parts[1]) + parts[2]
    pick_lane = lax.broadcasted_iota(jnp.int32, row_values.shape, 0) == low_part[None, :]
    return jnp.sum(jnp.where(pick_lane, row_values, 0.0), axis=0).reshape(index.shape)


def solve(right_side, coupling, sinking):
    levels = right_side.shape[1]
    sink_col = sinking[:, None]
    zero_row = jnp.zeros_like(coupling[0])
    ratios = []
    partial_value = []
    ratio_prev = None
    part_prev = None
    for level in range(levels):
        lower_c = coupling[level - 1] if level > 0 else zero_row
        upper_c = coupling[level] if level < levels - 1 else zero_row
        diagonal = 1.0 + lower_c[None] + upper_c[None] + sink_col
        if level == 0:
            pivot = diagonal
            part_now = right_side[:, level] / pivot
        else:
            pivot = diagonal + lower_c[None] * ratio_prev
            part_now = (right_side[:, level] + lower_c[None] * part_prev) / pivot
        if level < levels - 1:
            ratio_now = -(upper_c[None] + sink_col) / pivot
        else:
            ratio_now = jnp.zeros_like(pivot)
        ratios.append(ratio_now)
        partial_value.append(part_now)
        ratio_prev = ratio_now
        part_prev = part_now
    result = [None] * levels
    result[levels - 1] = partial_value[levels - 1]
    for level in range(levels - 2, -1, -1):
        result[level] = partial_value[level] - ratios[level] * result[level + 1]
    return jnp.stack(result, axis=1)


def on_device(
    land_wind,
    land_moist,
    texture,
    land_index,
    erod_map,
    mass_frac,
    blast_table,
    dest_tile,
    regrid_w,
    atm_state,
    dust_mix,
    mixing,
    settle,
):
    high = lax.Precision.HIGHEST
    nblocks, ncells = land_wind.shape
    columns = atm_state.shape[2]
    nbins = blast_table.shape[1]
    devices = lax.axis_size(("sec", "tile"))
    state = solve(atm_state, mixing, jnp.zeros((3,), jnp.float32))
    speed = jnp.sqrt(state[0, 0] ** 2 + state[1, 0] ** 2 + 0.25)
    surface = jnp.stack([speed, state[2, 0]]).astype(jnp.bfloat16).reshape(1, 2 * columns)
    spread = jnp.broadcast_to(surface, (devices, 2 * columns))
    gathered = lax.all_to_all(spread, ("sec", "tile"), split_axis=0, concat_axis=0, tiled=True)
    base_thresh = threshold_table(mass_frac.shape[1])
    erodible = lookup(erod_map, land_index)
    emission = emit(land_wind, land_moist, texture, erodible, mass_frac, blast_table, base_thresh)
    partial_flux = jnp.einsum(
        "gkl,gla->gka", emission, regrid_w, preferred_element_type=jnp.float32
    )
    flat_flux = partial_flux.reshape(nblocks, nbins * columns)
    targets = dest_tile[:, 0]
    onehot = (targets[:, None] == jnp.arange(devices)[None, :]).astype(jnp.float32)
    capacity = max(2, 2 * nblocks // devices)
    before = jnp.cumsum(onehot, axis=0) - onehot
    ranking = jnp.sum(before * onehot, axis=1).astype(jnp.int32)
    slot_of = targets * capacity + ranking
    placing = (jnp.arange(devices * capacity)[:, None] == slot_of[None, :]).astype(jnp.float32)
    outgoing = jnp.dot(placing, flat_flux, precision=high).reshape(
        devices, capacity * nbins * columns
    )
    incoming = lax.all_to_all(
        outgoing.astype(jnp.bfloat16), ("sec", "tile"), split_axis=0, concat_axis=0, tiled=True
    ).astype(outgoing.dtype)
    flux = jnp.sum(incoming.reshape(devices * capacity, nbins, columns), axis=0)
    flux = flux * (float(columns) / float(ncells * nblocks))
    loaded = dust_mix.at[:, 0, :].add(flux)
    dust_out = solve(loaded, mixing, settle)
    picked = jnp.dot(onehot.astype(jnp.bfloat16), gathered, preferred_element_type=jnp.float32)
    picked = picked.astype(jnp.bfloat16).reshape(nblocks, 2, columns)
    numer = jnp.einsum("gla,gka->kgl", regrid_w, picked, preferred_element_type=jnp.float32)
    denom = jnp.sum(regrid_w, axis=2, dtype=jnp.float32)
    land_fields = jnp.stack([numer[0] / denom, 0.5 * land_moist + 0.5 * numer[1] / denom])
    return (land_fields, dust_out)


def solution(mesh):
    in_specs = (
        P(("sec", "tile"), None),
        P(("sec", "tile"), None),
        P(("sec", "tile"), None),
        P(("sec", "tile"), None),
        P(("sec", "tile")),
        P(),
        P(),
        P(("sec", "tile"), None),
        P(("sec", "tile"), None, None),
        P(None, None, ("sec", "tile")),
        P(None, None, ("sec", "tile")),
        P(None, ("sec", "tile")),
        P(),
    )
    out_specs = (P(None, ("sec", "tile"), None), P(None, None, ("sec", "tile")))
    return jax.shard_map(
        on_device, mesh=mesh, in_specs=in_specs, out_specs=out_specs, check_vma=False
    )
```

```python
import jax
import jax.numpy as jnp
from jax import lax
from jax.sharding import PartitionSpec as P


def threshold_table(count):
    diameter = 4e-05 * jnp.power(jnp.float32(1.35), jnp.arange(count).astype(jnp.float32))
    return jnp.sqrt(0.0123 * (2160.0 * 9.81 * diameter + 0.0003 / (1.227 * diameter)))


def emit(wind_rows, moist_rows, texture_rows, erodible, mass_frac, blast_table, base_thresh):
    high = lax.Precision.HIGHEST
    thresh = base_thresh[:, None, None] * jnp.sqrt(1.0 + 12.1 * moist_rows)[None]
    classes = jnp.arange(mass_frac.shape[0])
    onehot = (texture_rows[None] == classes[:, None, None]).astype(jnp.float32)
    fraction = jnp.einsum("tb,tnl->bnl", mass_frac, onehot, precision=high)
    speed = wind_rows[None]
    salt = (
        40.0
        * fraction
        * erodible[None]
        * (speed + thresh)
        * jnp.maximum(speed * speed - thresh * thresh, 0.0)
    )
    blasted = jnp.einsum("tkb,bnl->tknl", blast_table, salt, precision=high)
    emission = jnp.sum(blasted * onehot[:, None], axis=0)
    return jnp.transpose(emission, (1, 0, 2)).astype(jnp.bfloat16)


def lookup(table, index):
    rows = table.shape[0] // 128
    flat = index.reshape(-1)
    high_part = flat // 128
    low_part = flat % 128
    pick_row = (lax.broadcasted_iota(jnp.int32, (rows, flat.shape[0]), 0) == high_part[None, :]).astype(jnp.bfloat16)
    grid = table.reshape(rows, 128)
    first_wide = lax.reduce_precision(grid, exponent_bits=8, mantissa_bits=7)
    rest = grid - first_wide
    second_wide = lax.reduce_precision(rest, exponent_bits=8, mantissa_bits=7)
    first = first_wide.astype(jnp.bfloat16)
    second = second_wide.astype(jnp.bfloat16)
    third = (rest - second_wide).astype(jnp.bfloat16)
    dims = (((0,), (0,)), ((), ()))
    parts = [lax.dot_general(p, pick_row, dims, preferred_element_type=jnp.float32) for p in (first, second, third)]
    row_values = (parts[0] + parts[1]) + parts[2]
    pick_lane = lax.broadcasted_iota(jnp.int32, row_values.shape, 0) == low_part[None, :]
    return jnp.sum(jnp.where(pick_lane, row_values, 0.0), axis=0).reshape(index.shape)


def solve(right_side, coupling, sinking):
    levels = right_side.shape[1]
    sink_col = sinking[:, None]
    zero_row = jnp.zeros_like(coupling[0])
    ratios = []
    partial_value = []
    ratio_prev = None
    part_prev = None
    for level in range(levels):
        lower_c = coupling[level - 1] if level > 0 else zero_row
        upper_c = coupling[level] if level < levels - 1 else zero_row
        diagonal = 1.0 + lower_c[None] + upper_c[None] + sink_col
        if level == 0:
            pivot = diagonal
            part_now = right_side[:, level] / pivot
        else:
            pivot = diagonal + lower_c[None] * ratio_prev
            part_now = (right_side[:, level] + lower_c[None] * part_prev) / pivot
        if level < levels - 1:
            ratio_now = -(upper_c[None] + sink_col) / pivot
        else:
            ratio_now = jnp.zeros_like(pivot)
        ratios.append(ratio_now)
        partial_value.append(part_now)
        ratio_prev = ratio_now
        part_prev = part_now
    result = [None] * levels
    result[levels - 1] = partial_value[levels - 1]
    for level in range(levels - 2, -1, -1):
        result[level] = partial_value[level] - ratios[level] * result[level + 1]
    return jnp.stack(result, axis=1)


def on_device(
    land_wind,
    land_moist,
    texture,
    land_index,
    erod_map,
    mass_frac,
    blast_table,
    dest_tile,
    regrid_w,
    atm_state,
    dust_mix,
    mixing,
    settle,
):
    high = lax.Precision.HIGHEST
    nblocks, ncells = land_wind.shape
    columns = atm_state.shape[2]
    nbins = blast_table.shape[1]
    devices = lax.axis_size(("sec", "tile"))
    state = solve(atm_state, mixing, jnp.zeros((3,), jnp.float32))
    speed = jnp.sqrt(state[0, 0] ** 2 + state[1, 0] ** 2 + 0.25)
    surface = jnp.stack([speed, state[2, 0]]).astype(jnp.bfloat16).reshape(1, 2 * columns)
    spread = jnp.broadcast_to(surface, (devices, 2 * columns))
    gathered = lax.all_to_all(spread, ("sec", "tile"), split_axis=0, concat_axis=0, tiled=True)
    base_thresh = threshold_table(mass_frac.shape[1])
    erodible = lookup(erod_map, land_index)
    emission = emit(land_wind, land_moist, texture, erodible, mass_frac, blast_table, base_thresh)
    partial_flux = jnp.einsum(
        "gkl,gla->gka", emission, regrid_w, preferred_element_type=jnp.float32
    )
    flat_flux = partial_flux.reshape(nblocks, nbins * columns)
    targets = dest_tile[:, 0]
    onehot = (targets[:, None] == jnp.arange(devices)[None, :]).astype(jnp.float32)
    dims = (((0,), (0,)), ((), ()))
    outgoing = lax.dot_general(onehot, flat_flux, dims, precision=high)
    incoming = lax.all_to_all(
        outgoing.astype(jnp.bfloat16), ("sec", "tile"), split_axis=0, concat_axis=0, tiled=True
    )
    flux = jnp.sum(incoming.astype(jnp.float32), axis=0).reshape(nbins, columns)
    flux = flux * (float(columns) / float(ncells * nblocks))
    loaded = dust_mix.at[:, 0, :].add(flux)
    dust_out = solve(loaded, mixing, settle)
    picked = jnp.dot(onehot.astype(jnp.bfloat16), gathered, preferred_element_type=jnp.float32)
    picked = picked.astype(jnp.bfloat16).reshape(nblocks, 2, columns)
    picked = jnp.concatenate([picked, jnp.ones((nblocks, 1, columns), jnp.bfloat16)], axis=1)
    numer = jnp.einsum("gla,gka->kgl", regrid_w, picked, preferred_element_type=jnp.float32)
    denom = numer[2]
    land_fields = jnp.stack([numer[0] / denom, 0.5 * land_moist + 0.5 * numer[1] / denom])
    return (land_fields, dust_out)


def solution(mesh):
    in_specs = (
        P(("sec", "tile"), None),
        P(("sec", "tile"), None),
        P(("sec", "tile"), None),
        P(("sec", "tile"), None),
        P(("sec", "tile")),
        P(),
        P(),
        P(("sec", "tile"), None),
        P(("sec", "tile"), None, None),
        P(None, None, ("sec", "tile")),
        P(None, None, ("sec", "tile")),
        P(None, ("sec", "tile")),
        P(),
    )
    out_specs = (P(None, ("sec", "tile"), None), P(None, None, ("sec", "tile")))
    return jax.shard_map(
        on_device, mesh=mesh, in_specs=in_specs, out_specs=out_specs, check_vma=False
    )
```

```python
import jax
import jax.numpy as jnp
from jax import lax
from jax.sharding import PartitionSpec as P


def threshold_table(count):
    diameter = 4e-05 * jnp.power(jnp.float32(1.35), jnp.arange(count).astype(jnp.float32))
    return jnp.sqrt(0.0123 * (2160.0 * 9.81 * diameter + 0.0003 / (1.227 * diameter)))


def emit(wind_rows, moist_rows, texture_rows, erodible, mass_frac, blast_table, base_thresh):
    high = lax.Precision.HIGHEST
    thresh = base_thresh[:, None, None] * jnp.sqrt(1.0 + 12.1 * moist_rows)[None]
    classes = jnp.arange(mass_frac.shape[0])
    onehot = (texture_rows[None] == classes[:, None, None]).astype(jnp.float32)
    fraction = jnp.einsum("tb,tnl->bnl", mass_frac, onehot, precision=high)
    speed = wind_rows[None]
    salt = (
        40.0
        * fraction
        * erodible[None]
        * (speed + thresh)
        * jnp.maximum(speed * speed - thresh * thresh, 0.0)
    )
    blasted = jnp.einsum("tkb,bnl->tknl", blast_table, salt, precision=high)
    emission = jnp.sum(blasted * onehot[:, None], axis=0)
    return jnp.transpose(emission, (1, 0, 2)).astype(jnp.bfloat16)


def lookup(table, index):
    rows = table.shape[0] // 128
    flat = index.reshape(-1)
    high_part = flat // 128
    low_part = flat % 128
    pick_row = (lax.broadcasted_iota(jnp.int32, (rows, flat.shape[0]), 0) == high_part[None, :]).astype(jnp.bfloat16)
    grid = table.reshape(rows, 128)
    first_wide = lax.reduce_precision(grid, exponent_bits=8, mantissa_bits=7)
    rest = grid - first_wide
    second_wide = lax.reduce_precision(rest, exponent_bits=8, mantissa_bits=7)
    first = first_wide.astype(jnp.bfloat16)
    second = second_wide.astype(jnp.bfloat16)
    third = (rest - second_wide).astype(jnp.bfloat16)
    dims = (((0,), (0,)), ((), ()))
    parts = [lax.dot_general(p, pick_row, dims, preferred_element_type=jnp.float32) for p in (first, second, third)]
    row_values = (parts[0] + parts[1]) + parts[2]
    pick_lane = lax.broadcasted_iota(jnp.int32, row_values.shape, 0) == low_part[None, :]
    return jnp.sum(jnp.where(pick_lane, row_values, 0.0), axis=0).reshape(index.shape)


def solve(right_side, coupling, sinking):
    levels = right_side.shape[1]
    sink_col = sinking[:, None]
    zero_row = jnp.zeros_like(coupling[0])
    ratios = []
    partial_value = []
    ratio_prev = None
    part_prev = None
    for level in range(levels):
        lower_c = coupling[level - 1] if level > 0 else zero_row
        upper_c = coupling[level] if level < levels - 1 else zero_row
        diagonal = 1.0 + lower_c[None] + upper_c[None] + sink_col
        if level == 0:
            pivot = diagonal
            part_now = right_side[:, level] / pivot
        else:
            pivot = diagonal + lower_c[None] * ratio_prev
            part_now = (right_side[:, level] + lower_c[None] * part_prev) / pivot
        if level < levels - 1:
            ratio_now = -(upper_c[None] + sink_col) / pivot
        else:
            ratio_now = jnp.zeros_like(pivot)
        ratios.append(ratio_now)
        partial_value.append(part_now)
        ratio_prev = ratio_now
        part_prev = part_now
    result = [None] * levels
    result[levels - 1] = partial_value[levels - 1]
    for level in range(levels - 2, -1, -1):
        result[level] = partial_value[level] - ratios[level] * result[level + 1]
    return jnp.stack(result, axis=1)


def on_device(
    land_wind,
    land_moist,
    texture,
    land_index,
    erod_map,
    mass_frac,
    blast_table,
    dest_tile,
    regrid_w,
    atm_state,
    dust_mix,
    mixing,
    settle,
):
    high = lax.Precision.HIGHEST
    nblocks, ncells = land_wind.shape
    columns = atm_state.shape[2]
    nbins = blast_table.shape[1]
    devices = lax.axis_size(("sec", "tile"))
    state = solve(atm_state, mixing, jnp.zeros((3,), jnp.float32))
    speed = jnp.sqrt(state[0, 0] ** 2 + state[1, 0] ** 2 + 0.25)
    surface = jnp.stack([speed, state[2, 0]]).astype(jnp.bfloat16).reshape(1, 2 * columns)
    base_thresh = threshold_table(mass_frac.shape[1])
    erodible = lookup(erod_map, land_index)
    emission = emit(land_wind, land_moist, texture, erodible, mass_frac, blast_table, base_thresh)
    partial_flux = jnp.einsum(
        "gkl,gla->gka", emission, regrid_w, preferred_element_type=jnp.float32
    )
    flat_flux = partial_flux.reshape(nblocks, nbins * columns)
    targets = dest_tile[:, 0]
    onehot = (targets[:, None] == jnp.arange(devices)[None, :]).astype(jnp.float32)
    dims = (((0,), (0,)), ((), ()))
    outgoing = lax.dot_general(onehot, flat_flux, dims, precision=high)
    spread = jnp.broadcast_to(surface, (devices, 2 * columns))
    payload = jnp.concatenate([outgoing.astype(jnp.bfloat16), spread], axis=1)
    incoming = lax.all_to_all(payload, ("sec", "tile"), split_axis=0, concat_axis=0, tiled=True)
    flux = jnp.sum(incoming[:, : nbins * columns].astype(jnp.float32), axis=0).reshape(nbins, columns)
    gathered = incoming[:, nbins * columns :]
    flux = flux * (float(columns) / float(ncells * nblocks))
    loaded = dust_mix.at[:, 0, :].add(flux)
    dust_out = solve(loaded, mixing, settle)
    picked = jnp.dot(onehot.astype(jnp.bfloat16), gathered, preferred_element_type=jnp.float32)
    picked = picked.astype(jnp.bfloat16).reshape(nblocks, 2, columns)
    picked = jnp.concatenate([picked, jnp.ones((nblocks, 1, columns), jnp.bfloat16)], axis=1)
    numer = jnp.einsum("gla,gka->kgl", regrid_w, picked, preferred_element_type=jnp.float32)
    denom = numer[2]
    land_fields = jnp.stack([numer[0] / denom, 0.5 * land_moist + 0.5 * numer[1] / denom])
    return (land_fields, dust_out)


def solution(mesh):
    in_specs = (
        P(("sec", "tile"), None),
        P(("sec", "tile"), None),
        P(("sec", "tile"), None),
        P(("sec", "tile"), None),
        P(("sec", "tile")),
        P(),
        P(),
        P(("sec", "tile"), None),
        P(("sec", "tile"), None, None),
        P(None, None, ("sec", "tile")),
        P(None, None, ("sec", "tile")),
        P(None, ("sec", "tile")),
        P(),
    )
    out_specs = (P(None, ("sec", "tile"), None), P(None, None, ("sec", "tile")))
    return jax.shard_map(
        on_device, mesh=mesh, in_specs=in_specs, out_specs=out_specs, check_vma=False
    )
```

```python
import jax
import jax.numpy as jnp
from jax import lax
from jax.experimental import pallas as pl
from jax.sharding import PartitionSpec as P


def threshold_table(count):
    diameter = 4e-05 * jnp.power(jnp.float32(1.35), jnp.arange(count).astype(jnp.float32))
    return jnp.sqrt(0.0123 * (2160.0 * 9.81 * diameter + 0.0003 / (1.227 * diameter)))


def emit(wind_rows, moist_rows, texture_rows, erodible, mass_frac, blast_table, base_thresh):
    high = lax.Precision.HIGHEST
    thresh = base_thresh[:, None, None] * jnp.sqrt(1.0 + 12.1 * moist_rows)[None]
    classes = jnp.arange(mass_frac.shape[0])
    onehot = (texture_rows[None] == classes[:, None, None]).astype(jnp.float32)
    fraction = jnp.einsum("tb,tnl->bnl", mass_frac, onehot, precision=high)
    speed = wind_rows[None]
    salt = (
        40.0
        * fraction
        * erodible[None]
        * (speed + thresh)
        * jnp.maximum(speed * speed - thresh * thresh, 0.0)
    )
    blasted = jnp.einsum("tkb,bnl->tknl", blast_table, salt, precision=high)
    emission = jnp.sum(blasted * onehot[:, None], axis=0)
    return jnp.transpose(emission, (1, 0, 2)).astype(jnp.bfloat16)


def lookup_kernel(index_ref, parts_ref, out_ref):
    rows_per_step, lanes = index_ref.shape
    segments = parts_ref.shape[1]
    for r in range(rows_per_step):
        cell = index_ref[r : r + 1, :]
        high_part = cell // 128
        low_part = cell % 128
        pick_row = lax.broadcasted_iota(jnp.int32, (segments, lanes), 0) == high_part
        pick_row = jnp.where(pick_row, 1.0, 0.0).astype(jnp.bfloat16)
        products = jnp.dot(parts_ref[...], pick_row, preferred_element_type=jnp.float32)
        row_values = (products[0:128] + products[128:256]) + products[256:384]
        pick_lane = lax.broadcasted_iota(jnp.int32, (128, lanes), 0) == low_part
        out_ref[r : r + 1, :] = jnp.sum(jnp.where(pick_lane, row_values, 0.0), axis=0, keepdims=True)


def lookup(table, index):
    segments = table.shape[0] // 128
    grid = table.reshape(segments, 128)
    first_wide = lax.reduce_precision(grid, exponent_bits=8, mantissa_bits=7)
    rest = grid - first_wide
    second_wide = lax.reduce_precision(rest, exponent_bits=8, mantissa_bits=7)
    parts = jnp.concatenate(
        [first_wide.T, second_wide.T, (rest - second_wide).T], axis=0
    ).astype(jnp.bfloat16)
    rows, lanes = index.shape
    step = 8
    return pl.pallas_call(
        lookup_kernel,
        out_shape=jax.ShapeDtypeStruct((rows, lanes), jnp.float32),
        grid=(rows // step,),
        in_specs=[
            pl.BlockSpec((step, lanes), lambda i: (i, 0)),
            pl.BlockSpec((3 * 128, segments), lambda i: (0, 0)),
        ],
        out_specs=pl.BlockSpec((step, lanes), lambda i: (i, 0)),
        cost_estimate=pl.CostEstimate(
            flops=2 * 384 * segments * rows * lanes, transcendentals=0,
            bytes_accessed=8 * rows * lanes + 2 * 384 * segments,
        ),
    )(index, parts)

def solve(right_side, coupling, sinking):
    levels = right_side.shape[1]
    sink_col = sinking[:, None]
    zero_row = jnp.zeros_like(coupling[0])
    ratios = []
    partial_value = []
    ratio_prev = None
    part_prev = None
    for level in range(levels):
        lower_c = coupling[level - 1] if level > 0 else zero_row
        upper_c = coupling[level] if level < levels - 1 else zero_row
        diagonal = 1.0 + lower_c[None] + upper_c[None] + sink_col
        if level == 0:
            pivot = diagonal
            part_now = right_side[:, level] / pivot
        else:
            pivot = diagonal + lower_c[None] * ratio_prev
            part_now = (right_side[:, level] + lower_c[None] * part_prev) / pivot
        if level < levels - 1:
            ratio_now = -(upper_c[None] + sink_col) / pivot
        else:
            ratio_now = jnp.zeros_like(pivot)
        ratios.append(ratio_now)
        partial_value.append(part_now)
        ratio_prev = ratio_now
        part_prev = part_now
    result = [None] * levels
    result[levels - 1] = partial_value[levels - 1]
    for level in range(levels - 2, -1, -1):
        result[level] = partial_value[level] - ratios[level] * result[level + 1]
    return jnp.stack(result, axis=1)


def on_device(
    land_wind,
    land_moist,
    texture,
    land_index,
    erod_map,
    mass_frac,
    blast_table,
    dest_tile,
    regrid_w,
    atm_state,
    dust_mix,
    mixing,
    settle,
):
    high = lax.Precision.HIGHEST
    nblocks, ncells = land_wind.shape
    columns = atm_state.shape[2]
    nbins = blast_table.shape[1]
    devices = lax.axis_size(("sec", "tile"))
    state = solve(atm_state, mixing, jnp.zeros((3,), jnp.float32))
    speed = jnp.sqrt(state[0, 0] ** 2 + state[1, 0] ** 2 + 0.25)
    surface = jnp.stack([speed, state[2, 0]]).astype(jnp.bfloat16).reshape(1, 2 * columns)
    base_thresh = threshold_table(mass_frac.shape[1])
    erodible = lookup(erod_map, land_index)
    emission = emit(land_wind, land_moist, texture, erodible, mass_frac, blast_table, base_thresh)
    partial_flux = jnp.einsum(
        "gkl,gla->gka", emission, regrid_w, preferred_element_type=jnp.float32
    )
    flat_flux = partial_flux.reshape(nblocks, nbins * columns)
    targets = dest_tile[:, 0]
    onehot = (targets[:, None] == jnp.arange(devices)[None, :]).astype(jnp.float32)
    dims = (((0,), (0,)), ((), ()))
    outgoing = lax.dot_general(onehot, flat_flux, dims, precision=high)
    spread = jnp.broadcast_to(surface, (devices, 2 * columns))
    payload = jnp.concatenate([outgoing.astype(jnp.bfloat16), spread], axis=1)
    incoming = lax.all_to_all(payload, ("sec", "tile"), split_axis=0, concat_axis=0, tiled=True)
    flux = jnp.sum(incoming[:, : nbins * columns].astype(jnp.float32), axis=0).reshape(nbins, columns)
    gathered = incoming[:, nbins * columns :]
    flux = flux * (float(columns) / float(ncells * nblocks))
    loaded = dust_mix.at[:, 0, :].add(flux)
    dust_out = solve(loaded, mixing, settle)
    picked = jnp.dot(onehot.astype(jnp.bfloat16), gathered, preferred_element_type=jnp.float32)
    picked = picked.astype(jnp.bfloat16).reshape(nblocks, 2, columns)
    picked = jnp.concatenate([picked, jnp.ones((nblocks, 1, columns), jnp.bfloat16)], axis=1)
    numer = jnp.einsum("gla,gka->kgl", regrid_w, picked, preferred_element_type=jnp.float32)
    denom = numer[2]
    land_fields = jnp.stack([numer[0] / denom, 0.5 * land_moist + 0.5 * numer[1] / denom])
    return (land_fields, dust_out)


def solution(mesh):
    in_specs = (
        P(("sec", "tile"), None),
        P(("sec", "tile"), None),
        P(("sec", "tile"), None),
        P(("sec", "tile"), None),
        P(("sec", "tile")),
        P(),
        P(),
        P(("sec", "tile"), None),
        P(("sec", "tile"), None, None),
        P(None, None, ("sec", "tile")),
        P(None, None, ("sec", "tile")),
        P(None, ("sec", "tile")),
        P(),
    )
    out_specs = (P(None, ("sec", "tile"), None), P(None, None, ("sec", "tile")))
    return jax.shard_map(
        on_device, mesh=mesh, in_specs=in_specs, out_specs=out_specs, check_vma=False
    )
```

```python
import jax
import jax.numpy as jnp
from jax import lax
from jax.sharding import PartitionSpec as P


def threshold_table(count):
    diameter = 4e-05 * jnp.power(jnp.float32(1.35), jnp.arange(count).astype(jnp.float32))
    return jnp.sqrt(0.0123 * (2160.0 * 9.81 * diameter + 0.0003 / (1.227 * diameter)))


def emit(wind_rows, moist_rows, texture_rows, erodible, mass_frac, blast_table, base_thresh):
    high = lax.Precision.HIGHEST
    thresh = base_thresh[:, None, None] * jnp.sqrt(1.0 + 12.1 * moist_rows)[None]
    classes = jnp.arange(mass_frac.shape[0])
    onehot = (texture_rows[None] == classes[:, None, None]).astype(jnp.float32)
    fraction = jnp.einsum("tb,tnl->bnl", mass_frac, onehot, precision=high)
    speed = wind_rows[None]
    salt = (
        40.0
        * fraction
        * erodible[None]
        * (speed + thresh)
        * jnp.maximum(speed * speed - thresh * thresh, 0.0)
    )
    blasted = jnp.einsum("tkb,bnl->tknl", blast_table, salt, precision=high)
    emission = jnp.sum(blasted * onehot[:, None], axis=0)
    return jnp.transpose(emission, (1, 0, 2)).astype(jnp.bfloat16)


def lookup(table, index):
    rows = table.shape[0] // 128
    flat = index.reshape(-1)
    high_part = flat // 128
    low_part = flat % 128
    pick_row = (lax.broadcasted_iota(jnp.int32, (rows, flat.shape[0]), 0) == high_part[None, :]).astype(jnp.bfloat16)
    grid = table.reshape(rows, 128)
    first_wide = lax.reduce_precision(grid, exponent_bits=8, mantissa_bits=7)
    rest = grid - first_wide
    second_wide = lax.reduce_precision(rest, exponent_bits=8, mantissa_bits=7)
    first = first_wide.astype(jnp.bfloat16)
    second = second_wide.astype(jnp.bfloat16)
    third = (rest - second_wide).astype(jnp.bfloat16)
    dims = (((0,), (0,)), ((), ()))
    parts = [lax.dot_general(p, pick_row, dims, preferred_element_type=jnp.float32) for p in (first, second, third)]
    row_values = (parts[0] + parts[1]) + parts[2]
    pick_lane = lax.broadcasted_iota(jnp.int32, row_values.shape, 0) == low_part[None, :]
    return jnp.sum(jnp.where(pick_lane, row_values, 0.0), axis=0).reshape(index.shape)


def solve(right_side, coupling, sinking):
    levels = right_side.shape[1]
    sink_col = sinking[:, None]
    zero_row = jnp.zeros_like(coupling[0])
    ratios = []
    partial_value = []
    ratio_prev = None
    part_prev = None
    for level in range(levels):
        lower_c = coupling[level - 1] if level > 0 else zero_row
        upper_c = coupling[level] if level < levels - 1 else zero_row
        diagonal = 1.0 + lower_c[None] + upper_c[None] + sink_col
        if level == 0:
            pivot = diagonal
            part_now = right_side[:, level] / pivot
        else:
            pivot = diagonal + lower_c[None] * ratio_prev
            part_now = (right_side[:, level] + lower_c[None] * part_prev) / pivot
        if level < levels - 1:
            ratio_now = -(upper_c[None] + sink_col) / pivot
        else:
            ratio_now = jnp.zeros_like(pivot)
        ratios.append(ratio_now)
        partial_value.append(part_now)
        ratio_prev = ratio_now
        part_prev = part_now
    result = [None] * levels
    result[levels - 1] = partial_value[levels - 1]
    for level in range(levels - 2, -1, -1):
        result[level] = partial_value[level] - ratios[level] * result[level + 1]
    return jnp.stack(result, axis=1)


def on_device(
    land_wind,
    land_moist,
    texture,
    land_index,
    erod_map,
    mass_frac,
    blast_table,
    dest_tile,
    regrid_w,
    atm_state,
    dust_mix,
    mixing,
    settle,
):
    high = lax.Precision.HIGHEST
    nblocks, ncells = land_wind.shape
    columns = atm_state.shape[2]
    nbins = blast_table.shape[1]
    devices = lax.axis_size(("sec", "tile"))
    state = solve(atm_state, mixing, jnp.zeros((3,), jnp.float32))
    speed = jnp.sqrt(state[0, 0] ** 2 + state[1, 0] ** 2 + 0.25)
    surface = jnp.stack([speed, state[2, 0]]).astype(jnp.bfloat16).reshape(1, 2 * columns)
    base_thresh = threshold_table(mass_frac.shape[1])
    erodible = lookup(erod_map, land_index)
    emission = emit(land_wind, land_moist, texture, erodible, mass_frac, blast_table, base_thresh)
    partial_flux = jnp.einsum(
        "gkl,gla->gka", emission, regrid_w, preferred_element_type=jnp.float32
    )
    flat_flux = partial_flux.reshape(nblocks, nbins * columns)
    targets = dest_tile[:, 0]
    onehot = (targets[:, None] == jnp.arange(devices)[None, :]).astype(jnp.float32)
    dims = (((0,), (0,)), ((), ()))
    outgoing = lax.dot_general(onehot, flat_flux, dims, precision=high)
    spread = jnp.broadcast_to(surface, (devices, 2 * columns))
    payload = jnp.concatenate([outgoing.astype(jnp.bfloat16), spread], axis=1)
    pairs = lax.axis_size("sec")
    width = payload.shape[1]
    payload = payload.reshape(pairs, devices // pairs, width)
    payload = lax.all_to_all(payload, "tile", split_axis=1, concat_axis=1, tiled=True)
    incoming = lax.all_to_all(payload, "sec", split_axis=0, concat_axis=0, tiled=True)
    incoming = incoming.reshape(devices, width)
    flux = jnp.sum(incoming[:, : nbins * columns].astype(jnp.float32), axis=0).reshape(nbins, columns)
    gathered = incoming[:, nbins * columns :]
    flux = flux * (float(columns) / float(ncells * nblocks))
    loaded = dust_mix.at[:, 0, :].add(flux)
    dust_out = solve(loaded, mixing, settle)
    picked = jnp.dot(onehot.astype(jnp.bfloat16), gathered, preferred_element_type=jnp.float32)
    picked = picked.astype(jnp.bfloat16).reshape(nblocks, 2, columns)
    picked = jnp.concatenate([picked, jnp.ones((nblocks, 1, columns), jnp.bfloat16)], axis=1)
    numer = jnp.einsum("gla,gka->kgl", regrid_w, picked, preferred_element_type=jnp.float32)
    denom = numer[2]
    land_fields = jnp.stack([numer[0] / denom, 0.5 * land_moist + 0.5 * numer[1] / denom])
    return (land_fields, dust_out)


def solution(mesh):
    in_specs = (
        P(("sec", "tile"), None),
        P(("sec", "tile"), None),
        P(("sec", "tile"), None),
        P(("sec", "tile"), None),
        P(("sec", "tile")),
        P(),
        P(),
        P(("sec", "tile"), None),
        P(("sec", "tile"), None, None),
        P(None, None, ("sec", "tile")),
        P(None, None, ("sec", "tile")),
        P(None, ("sec", "tile")),
        P(),
    )
    out_specs = (P(None, ("sec", "tile"), None), P(None, None, ("sec", "tile")))
    return jax.shard_map(
        on_device, mesh=mesh, in_specs=in_specs, out_specs=out_specs, check_vma=False
    )
```

```python
import jax
import jax.numpy as jnp
from jax import lax
from jax.experimental import pallas as pl
from jax.sharding import PartitionSpec as P


def threshold_table(count):
    diameter = 4e-05 * jnp.power(jnp.float32(1.35), jnp.arange(count).astype(jnp.float32))
    return jnp.sqrt(0.0123 * (2160.0 * 9.81 * diameter + 0.0003 / (1.227 * diameter)))


def emit(wind_rows, moist_rows, texture_rows, erodible, mass_frac, blast_table, base_thresh):
    high = lax.Precision.HIGHEST
    thresh = base_thresh[:, None, None] * jnp.sqrt(1.0 + 12.1 * moist_rows)[None]
    classes = jnp.arange(mass_frac.shape[0])
    onehot = (texture_rows[None] == classes[:, None, None]).astype(jnp.float32)
    fraction = jnp.einsum("tb,tnl->bnl", mass_frac, onehot, precision=high)
    speed = wind_rows[None]
    salt = (
        40.0
        * fraction
        * erodible[None]
        * (speed + thresh)
        * jnp.maximum(speed * speed - thresh * thresh, 0.0)
    )
    blasted = jnp.einsum("tkb,bnl->tknl", blast_table, salt, precision=high)
    emission = jnp.sum(blasted * onehot[:, None], axis=0)
    return jnp.transpose(emission, (1, 0, 2)).astype(jnp.bfloat16)


def lookup(table, index):
    rows = table.shape[0] // 128
    flat = index.reshape(-1)
    high_part = flat // 128
    low_part = flat % 128
    pick_row = (lax.broadcasted_iota(jnp.int32, (rows, flat.shape[0]), 0) == high_part[None, :]).astype(jnp.bfloat16)
    grid = table.reshape(rows, 128)
    first_wide = lax.reduce_precision(grid, exponent_bits=8, mantissa_bits=7)
    rest = grid - first_wide
    second_wide = lax.reduce_precision(rest, exponent_bits=8, mantissa_bits=7)
    first = first_wide.astype(jnp.bfloat16)
    second = second_wide.astype(jnp.bfloat16)
    third = (rest - second_wide).astype(jnp.bfloat16)
    dims = (((0,), (0,)), ((), ()))
    parts = [lax.dot_general(p, pick_row, dims, preferred_element_type=jnp.float32) for p in (first, second, third)]
    row_values = (parts[0] + parts[1]) + parts[2]
    pick_lane = lax.broadcasted_iota(jnp.int32, row_values.shape, 0) == low_part[None, :]
    return jnp.sum(jnp.where(pick_lane, row_values, 0.0), axis=0).reshape(index.shape)


def solve(right_side, coupling, sinking):
    levels = right_side.shape[1]
    sink_col = sinking[:, None]
    zero_row = jnp.zeros_like(coupling[0])
    ratios = []
    partial_value = []
    ratio_prev = None
    part_prev = None
    for level in range(levels):
        lower_c = coupling[level - 1] if level > 0 else zero_row
        upper_c = coupling[level] if level < levels - 1 else zero_row
        diagonal = 1.0 + lower_c[None] + upper_c[None] + sink_col
        if level == 0:
            pivot = diagonal
            part_now = right_side[:, level] / pivot
        else:
            pivot = diagonal + lower_c[None] * ratio_prev
            part_now = (right_side[:, level] + lower_c[None] * part_prev) / pivot
        if level < levels - 1:
            ratio_now = -(upper_c[None] + sink_col) / pivot
        else:
            ratio_now = jnp.zeros_like(pivot)
        ratios.append(ratio_now)
        partial_value.append(part_now)
        ratio_prev = ratio_now
        part_prev = part_now
    result = [None] * levels
    result[levels - 1] = partial_value[levels - 1]
    for level in range(levels - 2, -1, -1):
        result[level] = partial_value[level] - ratios[level] * result[level + 1]
    return jnp.stack(result, axis=1)


def back_kernel(dest_ref, gathered_ref, weights_ref, moist_ref, out_ref):
    blocks, _, columns = weights_ref.shape
    tiles = gathered_ref.shape[0]
    pick = lax.broadcasted_iota(jnp.int32, (blocks, tiles), 1) == dest_ref[...]
    pick = jnp.where(pick, 1.0, 0.0).astype(jnp.bfloat16)
    surfaces = jnp.dot(pick, gathered_ref[...], preferred_element_type=jnp.float32)
    rows = lax.broadcasted_iota(jnp.int32, (8, columns), 0)
    contract = (((1,), (1,)), ((), ()))
    for b in range(blocks):
        speed = surfaces[b : b + 1, :columns]
        humid = surfaces[b : b + 1, columns:]
        lhs = jnp.where(rows == 0, speed, jnp.where(rows == 1, humid, jnp.where(rows == 2, 1.0, 0.0)))
        sums = lax.dot_general(
            lhs.astype(jnp.bfloat16), weights_ref[b], contract, preferred_element_type=jnp.float32
        )
        denom = sums[2:3]
        out_ref[0, b : b + 1, :] = sums[0:1] / denom
        out_ref[1, b : b + 1, :] = 0.5 * moist_ref[b : b + 1, :] + 0.5 * (sums[1:2] / denom)


def regrid_back(dest_tile, gathered, regrid_w, land_moist):
    nblocks, ncells, columns = regrid_w.shape
    tiles, width = gathered.shape
    step = 16
    return pl.pallas_call(
        back_kernel,
        out_shape=jax.ShapeDtypeStruct((2, nblocks, ncells), jnp.float32),
        grid=(nblocks // step,),
        in_specs=[
            pl.BlockSpec((step, 1), lambda i: (i, 0)),
            pl.BlockSpec((tiles, width), lambda i: (0, 0)),
            pl.BlockSpec((step, ncells, columns), lambda i: (i, 0, 0)),
            pl.BlockSpec((step, ncells), lambda i: (i, 0)),
        ],
        out_specs=pl.BlockSpec((2, step, ncells), lambda i: (0, i, 0)),
        cost_estimate=pl.CostEstimate(
            flops=2 * 8 * columns * ncells * nblocks, transcendentals=0,
            bytes_accessed=2 * nblocks * ncells * columns + 12 * nblocks * ncells,
        ),
    )(dest_tile, gathered, regrid_w, land_moist)


def on_device(
    land_wind,
    land_moist,
    texture,
    land_index,
    erod_map,
    mass_frac,
    blast_table,
    dest_tile,
    regrid_w,
    atm_state,
    dust_mix,
    mixing,
    settle,
):
    high = lax.Precision.HIGHEST
    nblocks, ncells = land_wind.shape
    columns = atm_state.shape[2]
    nbins = blast_table.shape[1]
    devices = lax.axis_size(("sec", "tile"))
    state = solve(atm_state, mixing, jnp.zeros((3,), jnp.float32))
    speed = jnp.sqrt(state[0, 0] ** 2 + state[1, 0] ** 2 + 0.25)
    surface = jnp.stack([speed, state[2, 0]]).astype(jnp.bfloat16).reshape(1, 2 * columns)
    base_thresh = threshold_table(mass_frac.shape[1])
    erodible = lookup(erod_map, land_index)
    emission = emit(land_wind, land_moist, texture, erodible, mass_frac, blast_table, base_thresh)
    partial_flux = jnp.einsum(
        "gkl,gla->gka", emission, regrid_w, preferred_element_type=jnp.float32
    )
    flat_flux = partial_flux.reshape(nblocks, nbins * columns)
    targets = dest_tile[:, 0]
    onehot = (targets[:, None] == jnp.arange(devices)[None, :]).astype(jnp.float32)
    dims = (((0,), (0,)), ((), ()))
    outgoing = lax.dot_general(onehot, flat_flux, dims, precision=high)
    spread = jnp.broadcast_to(surface, (devices, 2 * columns))
    payload = jnp.concatenate([outgoing.astype(jnp.bfloat16), spread], axis=1)
    incoming = lax.all_to_all(payload, ("sec", "tile"), split_axis=0, concat_axis=0, tiled=True)
    flux = jnp.sum(incoming[:, : nbins * columns].astype(jnp.float32), axis=0).reshape(nbins, columns)
    gathered = incoming[:, nbins * columns :]
    flux = flux * (float(columns) / float(ncells * nblocks))
    loaded = dust_mix.at[:, 0, :].add(flux)
    dust_out = solve(loaded, mixing, settle)
    land_fields = regrid_back(dest_tile, gathered, regrid_w, land_moist)
    return (land_fields, dust_out)


def solution(mesh):
    in_specs = (
        P(("sec", "tile"), None),
        P(("sec", "tile"), None),
        P(("sec", "tile"), None),
        P(("sec", "tile"), None),
        P(("sec", "tile")),
        P(),
        P(),
        P(("sec", "tile"), None),
        P(("sec", "tile"), None, None),
        P(None, None, ("sec", "tile")),
        P(None, None, ("sec", "tile")),
        P(None, ("sec", "tile")),
        P(),
    )
    out_specs = (P(None, ("sec", "tile"), None), P(None, None, ("sec", "tile")))
    return jax.shard_map(
        on_device, mesh=mesh, in_specs=in_specs, out_specs=out_specs, check_vma=False
    )
```

```python
import jax
import jax.numpy as jnp
from jax import lax
from jax.sharding import PartitionSpec as P


def threshold_table(count):
    diameter = 4e-05 * jnp.power(jnp.float32(1.35), jnp.arange(count).astype(jnp.float32))
    return jnp.sqrt(0.0123 * (2160.0 * 9.81 * diameter + 0.0003 / (1.227 * diameter)))


def emit(wind_rows, moist_rows, texture_rows, erodible, mass_frac, blast_table, base_thresh):
    high = lax.Precision.HIGHEST
    thresh = base_thresh[:, None, None] * jnp.sqrt(1.0 + 12.1 * moist_rows)[None]
    classes = jnp.arange(mass_frac.shape[0])
    onehot = (texture_rows[None] == classes[:, None, None]).astype(jnp.float32)
    fraction = jnp.einsum("tb,tnl->bnl", mass_frac, onehot, precision=high)
    speed = wind_rows[None]
    salt = (
        40.0
        * fraction
        * erodible[None]
        * (speed + thresh)
        * jnp.maximum(speed * speed - thresh * thresh, 0.0)
    )
    blasted = jnp.einsum("tkb,bnl->tknl", blast_table, salt, precision=high)
    emission = jnp.sum(blasted * onehot[:, None], axis=0)
    return jnp.transpose(emission, (1, 0, 2)).astype(jnp.bfloat16)


def lookup(table, index):
    rows = table.shape[0] // 128
    flat = index.reshape(-1)
    high_part = flat // 128
    low_part = flat % 128
    grid = table.reshape(rows, 128)
    first_wide = lax.reduce_precision(grid, exponent_bits=8, mantissa_bits=7)
    rest = grid - first_wide
    second_wide = lax.reduce_precision(rest, exponent_bits=8, mantissa_bits=7)
    parts = jnp.concatenate([first_wide, second_wide, rest - second_wide], axis=0).astype(jnp.bfloat16)
    pick_row = lax.broadcasted_iota(jnp.int32, (3 * rows, flat.shape[0]), 0) % rows == high_part[None, :]
    pick_row = pick_row.astype(jnp.bfloat16)
    dims = (((0,), (0,)), ((), ()))
    row_values = lax.dot_general(parts, pick_row, dims, preferred_element_type=jnp.float32)
    pick_lane = lax.broadcasted_iota(jnp.int32, row_values.shape, 0) == low_part[None, :]
    return jnp.sum(jnp.where(pick_lane, row_values, 0.0), axis=0).reshape(index.shape)

def solve(right_side, coupling, sinking):
    levels = right_side.shape[1]
    sink_col = sinking[:, None]
    zero_row = jnp.zeros_like(coupling[0])
    ratios = []
    partial_value = []
    ratio_prev = None
    part_prev = None
    for level in range(levels):
        lower_c = coupling[level - 1] if level > 0 else zero_row
        upper_c = coupling[level] if level < levels - 1 else zero_row
        diagonal = 1.0 + lower_c[None] + upper_c[None] + sink_col
        if level == 0:
            pivot = diagonal
            part_now = right_side[:, level] / pivot
        else:
            pivot = diagonal + lower_c[None] * ratio_prev
            part_now = (right_side[:, level] + lower_c[None] * part_prev) / pivot
        if level < levels - 1:
            ratio_now = -(upper_c[None] + sink_col) / pivot
        else:
            ratio_now = jnp.zeros_like(pivot)
        ratios.append(ratio_now)
        partial_value.append(part_now)
        ratio_prev = ratio_now
        part_prev = part_now
    result = [None] * levels
    result[levels - 1] = partial_value[levels - 1]
    for level in range(levels - 2, -1, -1):
        result[level] = partial_value[level] - ratios[level] * result[level + 1]
    return jnp.stack(result, axis=1)


def on_device(
    land_wind,
    land_moist,
    texture,
    land_index,
    erod_map,
    mass_frac,
    blast_table,
    dest_tile,
    regrid_w,
    atm_state,
    dust_mix,
    mixing,
    settle,
):
    high = lax.Precision.HIGHEST
    nblocks, ncells = land_wind.shape
    columns = atm_state.shape[2]
    nbins = blast_table.shape[1]
    devices = lax.axis_size(("sec", "tile"))
    state = solve(atm_state, mixing, jnp.zeros((3,), jnp.float32))
    speed = jnp.sqrt(state[0, 0] ** 2 + state[1, 0] ** 2 + 0.25)
    surface = jnp.stack([speed, state[2, 0]]).astype(jnp.bfloat16).reshape(1, 2 * columns)
    base_thresh = threshold_table(mass_frac.shape[1])
    erodible = lookup(erod_map, land_index)
    emission = emit(land_wind, land_moist, texture, erodible, mass_frac, blast_table, base_thresh)
    partial_flux = jnp.einsum(
        "gkl,gla->gka", emission, regrid_w, preferred_element_type=jnp.float32
    )
    flat_flux = partial_flux.reshape(nblocks, nbins * columns)
    targets = dest_tile[:, 0]
    onehot = (targets[:, None] == jnp.arange(devices)[None, :]).astype(jnp.float32)
    dims = (((0,), (0,)), ((), ()))
    outgoing = lax.dot_general(onehot, flat_flux, dims, precision=high)
    spread = jnp.broadcast_to(surface, (devices, 2 * columns))
    payload = jnp.concatenate([outgoing.astype(jnp.bfloat16), spread], axis=1)
    incoming = lax.all_to_all(payload, ("sec", "tile"), split_axis=0, concat_axis=0, tiled=True)
    flux = jnp.sum(incoming[:, : nbins * columns].astype(jnp.float32), axis=0).reshape(nbins, columns)
    gathered = incoming[:, nbins * columns :]
    flux = flux * (float(columns) / float(ncells * nblocks))
    loaded = dust_mix.at[:, 0, :].add(flux)
    dust_out = solve(loaded, mixing, settle)
    picked = jnp.dot(onehot.astype(jnp.bfloat16), gathered, preferred_element_type=jnp.float32)
    picked = picked.astype(jnp.bfloat16).reshape(nblocks, 2, columns)
    picked = jnp.concatenate([picked, jnp.ones((nblocks, 1, columns), jnp.bfloat16)], axis=1)
    numer = jnp.einsum("gla,gka->kgl", regrid_w, picked, preferred_element_type=jnp.float32)
    denom = numer[2]
    land_fields = jnp.stack([numer[0] / denom, 0.5 * land_moist + 0.5 * numer[1] / denom])
    return (land_fields, dust_out)


def solution(mesh):
    in_specs = (
        P(("sec", "tile"), None),
        P(("sec", "tile"), None),
        P(("sec", "tile"), None),
        P(("sec", "tile"), None),
        P(("sec", "tile")),
        P(),
        P(),
        P(("sec", "tile"), None),
        P(("sec", "tile"), None, None),
        P(None, None, ("sec", "tile")),
        P(None, None, ("sec", "tile")),
        P(None, ("sec", "tile")),
        P(),
    )
    out_specs = (P(None, ("sec", "tile"), None), P(None, None, ("sec", "tile")))
    return jax.shard_map(
        on_device, mesh=mesh, in_specs=in_specs, out_specs=out_specs, check_vma=False
    )
```

```python
import jax
import jax.numpy as jnp
from jax import lax
from jax.sharding import PartitionSpec as P


def threshold_table(count):
    diameter = 4e-05 * jnp.power(jnp.float32(1.35), jnp.arange(count).astype(jnp.float32))
    return jnp.sqrt(0.0123 * (2160.0 * 9.81 * diameter + 0.0003 / (1.227 * diameter)))


def emit(wind_rows, moist_rows, texture_rows, erodible, mass_frac, blast_table, base_thresh):
    high = lax.Precision.HIGHEST
    thresh = base_thresh[:, None, None] * jnp.sqrt(1.0 + 12.1 * moist_rows)[None]
    classes = jnp.arange(mass_frac.shape[0])
    onehot = (texture_rows[None] == classes[:, None, None]).astype(jnp.float32)
    fraction = jnp.einsum("tb,tnl->bnl", mass_frac, onehot, precision=high)
    speed = wind_rows[None]
    salt = (
        40.0
        * fraction
        * erodible[None]
        * (speed + thresh)
        * jnp.maximum(speed * speed - thresh * thresh, 0.0)
    )
    blasted = jnp.einsum("tkb,bnl->tknl", blast_table, salt, precision=high)
    emission = jnp.sum(blasted * onehot[:, None], axis=0)
    return jnp.transpose(emission, (1, 0, 2)).astype(jnp.bfloat16)


def lookup(table, index):
    rows = table.shape[0] // 128
    flat = index.reshape(-1)
    high_part = flat // 128
    low_part = flat % 128
    grid = table.reshape(rows, 128)
    first_wide = lax.reduce_precision(grid, exponent_bits=8, mantissa_bits=7)
    rest = grid - first_wide
    second_wide = lax.reduce_precision(rest, exponent_bits=8, mantissa_bits=7)
    parts = jnp.concatenate([first_wide, second_wide, rest - second_wide], axis=0).astype(jnp.bfloat16)
    dims = (((0,), (0,)), ((), ()))
    halves = []
    for high_half, low_half in zip(jnp.split(high_part, 2), jnp.split(low_part, 2)):
        pick_row = lax.broadcasted_iota(jnp.int32, (3 * rows, high_half.shape[0]), 0) % rows == high_half[None, :]
        pick_row = pick_row.astype(jnp.bfloat16)
        row_values = lax.dot_general(parts, pick_row, dims, preferred_element_type=jnp.float32)
        pick_lane = lax.broadcasted_iota(jnp.int32, row_values.shape, 0) == low_half[None, :]
        halves.append(jnp.sum(jnp.where(pick_lane, row_values, 0.0), axis=0))
    return jnp.concatenate(halves).reshape(index.shape)

def solve(right_side, coupling, sinking):
    levels = right_side.shape[1]
    sink_col = sinking[:, None]
    zero_row = jnp.zeros_like(coupling[0])
    ratios = []
    partial_value = []
    ratio_prev = None
    part_prev = None
    for level in range(levels):
        lower_c = coupling[level - 1] if level > 0 else zero_row
        upper_c = coupling[level] if level < levels - 1 else zero_row
        diagonal = 1.0 + lower_c[None] + upper_c[None] + sink_col
        if level == 0:
            pivot = diagonal
            part_now = right_side[:, level] / pivot
        else:
            pivot = diagonal + lower_c[None] * ratio_prev
            part_now = (right_side[:, level] + lower_c[None] * part_prev) / pivot
        if level < levels - 1:
            ratio_now = -(upper_c[None] + sink_col) / pivot
        else:
            ratio_now = jnp.zeros_like(pivot)
        ratios.append(ratio_now)
        partial_value.append(part_now)
        ratio_prev = ratio_now
        part_prev = part_now
    result = [None] * levels
    result[levels - 1] = partial_value[levels - 1]
    for level in range(levels - 2, -1, -1):
        result[level] = partial_value[level] - ratios[level] * result[level + 1]
    return jnp.stack(result, axis=1)


def on_device(
    land_wind,
    land_moist,
    texture,
    land_index,
    erod_map,
    mass_frac,
    blast_table,
    dest_tile,
    regrid_w,
    atm_state,
    dust_mix,
    mixing,
    settle,
):
    high = lax.Precision.HIGHEST
    nblocks, ncells = land_wind.shape
    columns = atm_state.shape[2]
    nbins = blast_table.shape[1]
    devices = lax.axis_size(("sec", "tile"))
    state = solve(atm_state, mixing, jnp.zeros((3,), jnp.float32))
    speed = jnp.sqrt(state[0, 0] ** 2 + state[1, 0] ** 2 + 0.25)
    surface = jnp.stack([speed, state[2, 0]]).astype(jnp.bfloat16).reshape(1, 2 * columns)
    base_thresh = threshold_table(mass_frac.shape[1])
    erodible = lookup(erod_map, land_index)
    emission = emit(land_wind, land_moist, texture, erodible, mass_frac, blast_table, base_thresh)
    partial_flux = jnp.einsum(
        "gkl,gla->gka", emission, regrid_w, preferred_element_type=jnp.float32
    )
    flat_flux = partial_flux.reshape(nblocks, nbins * columns)
    targets = dest_tile[:, 0]
    onehot = (targets[:, None] == jnp.arange(devices)[None, :]).astype(jnp.float32)
    dims = (((0,), (0,)), ((), ()))
    surface_row = jnp.concatenate(
        [jnp.zeros((1, nbins * columns), jnp.float32), surface.astype(jnp.float32)], axis=1
    )
    stacked = jnp.concatenate(
        [jnp.pad(flat_flux, ((0, 0), (0, 2 * columns))), surface_row], axis=0
    )
    placing = jnp.concatenate([onehot, jnp.ones((1, devices), jnp.float32)], axis=0)
    payload = lax.dot_general(placing, stacked, dims, precision=high).astype(jnp.bfloat16)
    incoming = lax.all_to_all(payload, ("sec", "tile"), split_axis=0, concat_axis=0, tiled=True)
    flux = jnp.sum(incoming[:, : nbins * columns].astype(jnp.float32), axis=0).reshape(nbins, columns)
    gathered = incoming[:, nbins * columns :]
    flux = flux * (float(columns) / float(ncells * nblocks))
    loaded = dust_mix.at[:, 0, :].add(flux)
    dust_out = solve(loaded, mixing, settle)
    picked = jnp.dot(onehot.astype(jnp.bfloat16), gathered, preferred_element_type=jnp.float32)
    picked = picked.astype(jnp.bfloat16).reshape(nblocks, 2, columns)
    picked = jnp.concatenate([picked, jnp.ones((nblocks, 1, columns), jnp.bfloat16)], axis=1)
    numer = jnp.einsum("gla,gka->kgl", regrid_w, picked, preferred_element_type=jnp.float32)
    denom = numer[2]
    land_fields = jnp.stack([numer[0] / denom, 0.5 * land_moist + 0.5 * numer[1] / denom])
    return (land_fields, dust_out)


def solution(mesh):
    in_specs = (
        P(("sec", "tile"), None),
        P(("sec", "tile"), None),
        P(("sec", "tile"), None),
        P(("sec", "tile"), None),
        P(("sec", "tile")),
        P(),
        P(),
        P(("sec", "tile"), None),
        P(("sec", "tile"), None, None),
        P(None, None, ("sec", "tile")),
        P(None, None, ("sec", "tile")),
        P(None, ("sec", "tile")),
        P(),
    )
    out_specs = (P(None, ("sec", "tile"), None), P(None, None, ("sec", "tile")))
    return jax.shard_map(
        on_device, mesh=mesh, in_specs=in_specs, out_specs=out_specs, check_vma=False
    )
```

```python
import jax
import jax.numpy as jnp
from jax import lax
from jax.sharding import PartitionSpec as P


def threshold_table(count):
    diameter = 4e-05 * jnp.power(jnp.float32(1.35), jnp.arange(count).astype(jnp.float32))
    return jnp.sqrt(0.0123 * (2160.0 * 9.81 * diameter + 0.0003 / (1.227 * diameter)))


def emit(wind_rows, moist_rows, texture_rows, erodible, mass_frac, blast_table, base_thresh):
    high = lax.Precision.HIGHEST
    thresh = base_thresh[:, None, None] * jnp.sqrt(1.0 + 12.1 * moist_rows)[None]
    classes = jnp.arange(mass_frac.shape[0])
    onehot = (texture_rows[None] == classes[:, None, None]).astype(jnp.float32)
    fraction = jnp.einsum("tb,tnl->bnl", mass_frac, onehot, precision=high)
    speed = wind_rows[None]
    salt = (
        40.0
        * fraction
        * erodible[None]
        * (speed + thresh)
        * jnp.maximum(speed * speed - thresh * thresh, 0.0)
    )
    blasted = jnp.einsum("tkb,bnl->tknl", blast_table, salt, precision=high)
    emission = jnp.sum(blasted * onehot[:, None], axis=0)
    return jnp.transpose(emission, (1, 0, 2)).astype(jnp.bfloat16)


def lookup(table, index):
    rows = table.shape[0] // 128
    flat = index.reshape(-1)
    high_part = flat // 128
    low_part = flat % 128
    pick_row = (lax.broadcasted_iota(jnp.int32, (rows, flat.shape[0]), 0) == high_part[None, :]).astype(jnp.bfloat16)
    grid = table.reshape(rows, 128)
    first_wide = lax.reduce_precision(grid, exponent_bits=8, mantissa_bits=7)
    rest = grid - first_wide
    second_wide = lax.reduce_precision(rest, exponent_bits=8, mantissa_bits=7)
    first = first_wide.astype(jnp.bfloat16)
    second = second_wide.astype(jnp.bfloat16)
    third = (rest - second_wide).astype(jnp.bfloat16)
    dims = (((0,), (0,)), ((), ()))
    parts = [lax.dot_general(p, pick_row, dims, preferred_element_type=jnp.float32) for p in (first, second, third)]
    row_values = (parts[0] + parts[1]) + parts[2]
    pick_lane = lax.broadcasted_iota(jnp.int32, row_values.shape, 0) == low_part[None, :]
    return jnp.sum(jnp.where(pick_lane, row_values, 0.0), axis=0).reshape(index.shape)


def solve(right_side, coupling, sinking):
    levels = right_side.shape[1]
    sink_col = sinking[:, None]
    zero_row = jnp.zeros_like(coupling[0])
    ratios = []
    partial_value = []
    ratio_prev = None
    part_prev = None
    for level in range(levels):
        lower_c = coupling[level - 1] if level > 0 else zero_row
        upper_c = coupling[level] if level < levels - 1 else zero_row
        diagonal = 1.0 + lower_c[None] + upper_c[None] + sink_col
        if level == 0:
            pivot = diagonal
            part_now = right_side[:, level] / pivot
        else:
            pivot = diagonal + lower_c[None] * ratio_prev
            part_now = (right_side[:, level] + lower_c[None] * part_prev) / pivot
        if level < levels - 1:
            ratio_now = -(upper_c[None] + sink_col) / pivot
        else:
            ratio_now = jnp.zeros_like(pivot)
        ratios.append(ratio_now)
        partial_value.append(part_now)
        ratio_prev = ratio_now
        part_prev = part_now
    result = [None] * levels
    result[levels - 1] = partial_value[levels - 1]
    for level in range(levels - 2, -1, -1):
        result[level] = partial_value[level] - ratios[level] * result[level + 1]
    return jnp.stack(result, axis=1)


def on_device(
    land_wind,
    land_moist,
    texture,
    land_index,
    erod_map,
    mass_frac,
    blast_table,
    dest_tile,
    regrid_w,
    atm_state,
    dust_mix,
    mixing,
    settle,
):
    high = lax.Precision.HIGHEST
    nblocks, ncells = land_wind.shape
    columns = atm_state.shape[2]
    nbins = blast_table.shape[1]
    devices = lax.axis_size(("sec", "tile"))
    state = solve(atm_state, mixing, jnp.zeros((3,), jnp.float32))
    speed = jnp.sqrt(state[0, 0] ** 2 + state[1, 0] ** 2 + 0.25)
    surface = jnp.stack([speed, state[2, 0]]).astype(jnp.bfloat16).reshape(1, 2 * columns)
    base_thresh = threshold_table(mass_frac.shape[1])
    erodible = lookup(erod_map, land_index)
    emission = emit(land_wind, land_moist, texture, erodible, mass_frac, blast_table, base_thresh)
    partial_flux = jnp.einsum(
        "gkl,gla->gka", emission, regrid_w, preferred_element_type=jnp.float32
    )
    flat_flux = partial_flux.reshape(nblocks, nbins * columns)
    targets = dest_tile[:, 0]
    onehot = (targets[:, None] == jnp.arange(devices)[None, :]).astype(jnp.float32)
    dims = (((0,), (0,)), ((), ()))
    outgoing = lax.dot_general(onehot, flat_flux, dims, precision=high)
    spread = jnp.broadcast_to(surface, (devices, 2 * columns))
    payload = jnp.concatenate([outgoing, spread.astype(jnp.float32)], axis=1)
    incoming = lax.all_to_all(payload, ("sec", "tile"), split_axis=0, concat_axis=0, tiled=True)
    flux = jnp.sum(incoming[:, : nbins * columns].astype(jnp.float32), axis=0).reshape(nbins, columns)
    gathered = incoming[:, nbins * columns :].astype(jnp.bfloat16)
    flux = flux * (float(columns) / float(ncells * nblocks))
    loaded = dust_mix.at[:, 0, :].add(flux)
    dust_out = solve(loaded, mixing, settle)
    picked = jnp.dot(onehot.astype(jnp.bfloat16), gathered, preferred_element_type=jnp.float32)
    picked = picked.astype(jnp.bfloat16).reshape(nblocks, 2, columns)
    picked = jnp.concatenate([picked, jnp.ones((nblocks, 1, columns), jnp.bfloat16)], axis=1)
    numer = jnp.einsum("gla,gka->kgl", regrid_w, picked, preferred_element_type=jnp.float32)
    denom = numer[2]
    land_fields = jnp.stack([numer[0] / denom, 0.5 * land_moist + 0.5 * numer[1] / denom])
    return (land_fields, dust_out)


def solution(mesh):
    in_specs = (
        P(("sec", "tile"), None),
        P(("sec", "tile"), None),
        P(("sec", "tile"), None),
        P(("sec", "tile"), None),
        P(("sec", "tile")),
        P(),
        P(),
        P(("sec", "tile"), None),
        P(("sec", "tile"), None, None),
        P(None, None, ("sec", "tile")),
        P(None, None, ("sec", "tile")),
        P(None, ("sec", "tile")),
        P(),
    )
    out_specs = (P(None, ("sec", "tile"), None), P(None, None, ("sec", "tile")))
    return jax.shard_map(
        on_device, mesh=mesh, in_specs=in_specs, out_specs=out_specs, check_vma=False
    )
```

```python
import jax
import jax.numpy as jnp
from jax import lax
from jax.sharding import PartitionSpec as P


def threshold_table(count):
    diameter = 4e-05 * jnp.power(jnp.float32(1.35), jnp.arange(count).astype(jnp.float32))
    return jnp.sqrt(0.0123 * (2160.0 * 9.81 * diameter + 0.0003 / (1.227 * diameter)))


def emit(wind_rows, moist_rows, texture_rows, erodible, mass_frac, blast_table, base_thresh):
    high = lax.Precision.HIGHEST
    thresh = base_thresh[:, None, None] * jnp.sqrt(1.0 + 12.1 * moist_rows)[None]
    classes = jnp.arange(mass_frac.shape[0])
    onehot = (texture_rows[None] == classes[:, None, None]).astype(jnp.float32)
    fraction = jnp.einsum("tb,tnl->bnl", mass_frac, onehot, precision=high)
    speed = wind_rows[None]
    salt = (
        40.0
        * fraction
        * erodible[None]
        * (speed + thresh)
        * jnp.maximum(speed * speed - thresh * thresh, 0.0)
    )
    blasted = jnp.einsum("tkb,bnl->tknl", blast_table, salt, precision=high)
    emission = jnp.sum(blasted * onehot[:, None], axis=0)
    return jnp.transpose(emission, (1, 0, 2)).astype(jnp.bfloat16)


def lookup(table, index):
    rows = table.shape[0] // 128
    flat = index.reshape(-1)
    high_part = flat // 128
    low_part = flat % 128
    pick_row = (lax.broadcasted_iota(jnp.int32, (rows, flat.shape[0]), 0) == high_part[None, :]).astype(jnp.bfloat16)
    grid = table.reshape(rows, 128)
    first_wide = lax.reduce_precision(grid, exponent_bits=8, mantissa_bits=7)
    rest = grid - first_wide
    second_wide = lax.reduce_precision(rest, exponent_bits=8, mantissa_bits=7)
    first = first_wide.astype(jnp.bfloat16)
    second = second_wide.astype(jnp.bfloat16)
    third = (rest - second_wide).astype(jnp.bfloat16)
    dims = (((0,), (0,)), ((), ()))
    parts = [lax.dot_general(p, pick_row, dims, preferred_element_type=jnp.float32) for p in (first, second, third)]
    row_values = (parts[0] + parts[1]) + parts[2]
    pick_lane = lax.broadcasted_iota(jnp.int32, row_values.shape, 0) == low_part[None, :]
    return jnp.sum(jnp.where(pick_lane, row_values, 0.0), axis=0).reshape(index.shape)


def solve(right_side, coupling, sinking):
    levels = right_side.shape[1]
    sink_col = sinking[:, None]
    zero_row = jnp.zeros_like(coupling[0])
    ratios = []
    partial_value = []
    ratio_prev = None
    part_prev = None
    for level in range(levels):
        lower_c = coupling[level - 1] if level > 0 else zero_row
        upper_c = coupling[level] if level < levels - 1 else zero_row
        diagonal = 1.0 + lower_c[None] + upper_c[None] + sink_col
        if level == 0:
            pivot = diagonal
            part_now = right_side[:, level] / pivot
        else:
            pivot = diagonal + lower_c[None] * ratio_prev
            part_now = (right_side[:, level] + lower_c[None] * part_prev) / pivot
        if level < levels - 1:
            ratio_now = -(upper_c[None] + sink_col) / pivot
        else:
            ratio_now = jnp.zeros_like(pivot)
        ratios.append(ratio_now)
        partial_value.append(part_now)
        ratio_prev = ratio_now
        part_prev = part_now
    result = [None] * levels
    result[levels - 1] = partial_value[levels - 1]
    for level in range(levels - 2, -1, -1):
        result[level] = partial_value[level] - ratios[level] * result[level + 1]
    return jnp.stack(result, axis=1)


def on_device(
    land_wind,
    land_moist,
    texture,
    land_index,
    erod_map,
    mass_frac,
    blast_table,
    dest_tile,
    regrid_w,
    atm_state,
    dust_mix,
    mixing,
    settle,
):
    high = lax.Precision.HIGHEST
    nblocks, ncells = land_wind.shape
    columns = atm_state.shape[2]
    nbins = blast_table.shape[1]
    devices = lax.axis_size(("sec", "tile"))
    state = solve(atm_state, mixing, jnp.zeros((3,), jnp.float32))
    speed = jnp.sqrt(state[0, 0] ** 2 + state[1, 0] ** 2 + 0.25)
    surface = jnp.stack([speed, state[2, 0]]).astype(jnp.bfloat16).reshape(1, 2 * columns)
    base_thresh = threshold_table(mass_frac.shape[1])
    erodible = lookup(erod_map, land_index)
    emission = emit(land_wind, land_moist, texture, erodible, mass_frac, blast_table, base_thresh)
    partial_flux = jnp.einsum(
        "gkl,gla->gka", emission, regrid_w, preferred_element_type=jnp.float32
    )
    flat_flux = partial_flux.reshape(nblocks, nbins * columns)
    targets = dest_tile[:, 0]
    onehot = (targets[:, None] == jnp.arange(devices)[None, :]).astype(jnp.float32)
    dims = (((0,), (0,)), ((), ()))
    outgoing = lax.dot_general(onehot, flat_flux, dims, precision=high)
    spread = jnp.broadcast_to(surface, (devices, 2 * columns))
    half = nbins * columns // 2
    payload = jnp.concatenate(
        [outgoing.astype(jnp.bfloat16).reshape(devices, 2, half), spread.reshape(devices, 2, columns)], axis=2
    )
    incoming = lax.all_to_all(payload, ("sec", "tile"), split_axis=0, concat_axis=0, tiled=True)
    flux = jnp.sum(incoming[:, :, :half].astype(jnp.float32), axis=0).reshape(nbins, columns)
    gathered = incoming[:, :, half:].reshape(devices, 2 * columns)
    flux = flux * (float(columns) / float(ncells * nblocks))
    loaded = dust_mix.at[:, 0, :].add(flux)
    dust_out = solve(loaded, mixing, settle)
    picked = jnp.dot(onehot.astype(jnp.bfloat16), gathered, preferred_element_type=jnp.float32)
    picked = picked.astype(jnp.bfloat16).reshape(nblocks, 2, columns)
    picked = jnp.concatenate([picked, jnp.ones((nblocks, 1, columns), jnp.bfloat16)], axis=1)
    numer = jnp.einsum("gla,gka->kgl", regrid_w, picked, preferred_element_type=jnp.float32)
    denom = numer[2]
    land_fields = jnp.stack([numer[0] / denom, 0.5 * land_moist + 0.5 * numer[1] / denom])
    return (land_fields, dust_out)


def solution(mesh):
    in_specs = (
        P(("sec", "tile"), None),
        P(("sec", "tile"), None),
        P(("sec", "tile"), None),
        P(("sec", "tile"), None),
        P(("sec", "tile")),
        P(),
        P(),
        P(("sec", "tile"), None),
        P(("sec", "tile"), None, None),
        P(None, None, ("sec", "tile")),
        P(None, None, ("sec", "tile")),
        P(None, ("sec", "tile")),
        P(),
    )
    out_specs = (P(None, ("sec", "tile"), None), P(None, None, ("sec", "tile")))
    return jax.shard_map(
        on_device, mesh=mesh, in_specs=in_specs, out_specs=out_specs, check_vma=False
    )
```

```python
import jax
import jax.numpy as jnp
from jax import lax
from jax.experimental import pallas as pl
from jax.experimental.pallas import tpu as pltpu
from jax.sharding import PartitionSpec as P


def threshold_table(count):
    diameter = 4e-05 * jnp.power(jnp.float32(1.35), jnp.arange(count).astype(jnp.float32))
    return jnp.sqrt(0.0123 * (2160.0 * 9.81 * diameter + 0.0003 / (1.227 * diameter)))


def emit(wind_rows, moist_rows, texture_rows, erodible, mass_frac, blast_table, base_thresh):
    high = lax.Precision.HIGHEST
    thresh = base_thresh[:, None, None] * jnp.sqrt(1.0 + 12.1 * moist_rows)[None]
    classes = jnp.arange(mass_frac.shape[0])
    onehot = (texture_rows[None] == classes[:, None, None]).astype(jnp.float32)
    fraction = jnp.einsum("tb,tnl->bnl", mass_frac, onehot, precision=high)
    speed = wind_rows[None]
    salt = (
        40.0
        * fraction
        * erodible[None]
        * (speed + thresh)
        * jnp.maximum(speed * speed - thresh * thresh, 0.0)
    )
    blasted = jnp.einsum("tkb,bnl->tknl", blast_table, salt, precision=high)
    emission = jnp.sum(blasted * onehot[:, None], axis=0)
    return jnp.transpose(emission, (1, 0, 2)).astype(jnp.bfloat16)


def lookup_kernel(index_ref, parts_ref, out_ref):
    rows_per_step, lanes = index_ref.shape
    segments = parts_ref.shape[1] // 3
    levels = lax.broadcasted_iota(jnp.int32, (segments, lanes), 0).astype(jnp.bfloat16)
    lane_rows = lax.broadcasted_iota(jnp.int32, (128, lanes), 0)
    one = jnp.ones((segments, lanes), jnp.bfloat16)
    zero = jnp.zeros((segments, lanes), jnp.bfloat16)
    for r in range(rows_per_step):
        cell = index_ref[r : r + 1, :]
        high_part = (cell // 128).astype(jnp.bfloat16)
        low_part = cell % 128
        pick_row = jnp.where(levels == high_part, one, zero)
        stacked = jnp.concatenate([pick_row, pick_row, pick_row], axis=0)
        row_values = jnp.dot(parts_ref[...], stacked, preferred_element_type=jnp.float32)
        pick_lane = lane_rows == low_part
        out_ref[r : r + 1, :] = jnp.sum(jnp.where(pick_lane, row_values, 0.0), axis=0, keepdims=True)


def lookup(table, index):
    segments = table.shape[0] // 128
    grid = table.reshape(segments, 128)
    first_wide = lax.reduce_precision(grid, exponent_bits=8, mantissa_bits=7)
    rest = grid - first_wide
    second_wide = lax.reduce_precision(rest, exponent_bits=8, mantissa_bits=7)
    parts = jnp.concatenate([first_wide, second_wide, rest - second_wide], axis=0).T.astype(jnp.bfloat16)
    rows, lanes = index.shape
    step = 8
    return pl.pallas_call(
        lookup_kernel,
        out_shape=jax.ShapeDtypeStruct((rows, lanes), jnp.float32),
        grid=(rows // step,),
        in_specs=[
            pl.BlockSpec((step, lanes), lambda i: (i, 0)),
            pl.BlockSpec((128, 3 * segments), lambda i: (0, 0)),
        ],
        out_specs=pl.BlockSpec((step, lanes), lambda i: (i, 0)),
        compiler_params=pltpu.CompilerParams(vmem_limit_bytes=8 * 1024 * 1024),
        cost_estimate=pl.CostEstimate(
            flops=2 * 384 * segments * rows * lanes, transcendentals=0,
            bytes_accessed=8 * rows * lanes + 768 * segments,
        ),
    )(index, parts)

def solve(right_side, coupling, sinking):
    levels = right_side.shape[1]
    sink_col = sinking[:, None]
    zero_row = jnp.zeros_like(coupling[0])
    ratios = []
    partial_value = []
    ratio_prev = None
    part_prev = None
    for level in range(levels):
        lower_c = coupling[level - 1] if level > 0 else zero_row
        upper_c = coupling[level] if level < levels - 1 else zero_row
        diagonal = 1.0 + lower_c[None] + upper_c[None] + sink_col
        if level == 0:
            pivot = diagonal
            part_now = right_side[:, level] / pivot
        else:
            pivot = diagonal + lower_c[None] * ratio_prev
            part_now = (right_side[:, level] + lower_c[None] * part_prev) / pivot
        if level < levels - 1:
            ratio_now = -(upper_c[None] + sink_col) / pivot
        else:
            ratio_now = jnp.zeros_like(pivot)
        ratios.append(ratio_now)
        partial_value.append(part_now)
        ratio_prev = ratio_now
        part_prev = part_now
    result = [None] * levels
    result[levels - 1] = partial_value[levels - 1]
    for level in range(levels - 2, -1, -1):
        result[level] = partial_value[level] - ratios[level] * result[level + 1]
    return jnp.stack(result, axis=1)


def on_device(
    land_wind,
    land_moist,
    texture,
    land_index,
    erod_map,
    mass_frac,
    blast_table,
    dest_tile,
    regrid_w,
    atm_state,
    dust_mix,
    mixing,
    settle,
):
    high = lax.Precision.HIGHEST
    nblocks, ncells = land_wind.shape
    columns = atm_state.shape[2]
    nbins = blast_table.shape[1]
    devices = lax.axis_size(("sec", "tile"))
    state = solve(atm_state, mixing, jnp.zeros((3,), jnp.float32))
    speed = jnp.sqrt(state[0, 0] ** 2 + state[1, 0] ** 2 + 0.25)
    surface = jnp.stack([speed, state[2, 0]]).astype(jnp.bfloat16).reshape(1, 2 * columns)
    base_thresh = threshold_table(mass_frac.shape[1])
    erodible = lookup(erod_map, land_index)
    emission = emit(land_wind, land_moist, texture, erodible, mass_frac, blast_table, base_thresh)
    partial_flux = jnp.einsum(
        "gkl,gla->gka", emission, regrid_w, preferred_element_type=jnp.float32
    )
    flat_flux = partial_flux.reshape(nblocks, nbins * columns)
    targets = dest_tile[:, 0]
    onehot = (targets[:, None] == jnp.arange(devices)[None, :]).astype(jnp.float32)
    dims = (((0,), (0,)), ((), ()))
    outgoing = lax.dot_general(onehot, flat_flux, dims, precision=high)
    spread = jnp.broadcast_to(surface, (devices, 2 * columns))
    half = nbins * columns // 2
    payload = jnp.concatenate(
        [outgoing.astype(jnp.bfloat16).reshape(devices, 2, half), spread.reshape(devices, 2, columns)], axis=2
    )
    incoming = lax.all_to_all(payload, ("sec", "tile"), split_axis=0, concat_axis=0, tiled=True)
    flux = jnp.sum(incoming[:, :, :half].astype(jnp.float32), axis=0).reshape(nbins, columns)
    gathered = incoming[:, :, half:].reshape(devices, 2 * columns)
    flux = flux * (float(columns) / float(ncells * nblocks))
    loaded = dust_mix.at[:, 0, :].add(flux)
    dust_out = solve(loaded, mixing, settle)
    picked = jnp.dot(onehot.astype(jnp.bfloat16), gathered, preferred_element_type=jnp.float32)
    picked = picked.astype(jnp.bfloat16).reshape(nblocks, 2, columns)
    picked = jnp.concatenate([picked, jnp.ones((nblocks, 1, columns), jnp.bfloat16)], axis=1)
    numer = jnp.einsum("gla,gka->kgl", regrid_w, picked, preferred_element_type=jnp.float32)
    denom = numer[2]
    land_fields = jnp.stack([numer[0] / denom, 0.5 * land_moist + 0.5 * numer[1] / denom])
    return (land_fields, dust_out)


def solution(mesh):
    in_specs = (
        P(("sec", "tile"), None),
        P(("sec", "tile"), None),
        P(("sec", "tile"), None),
        P(("sec", "tile"), None),
        P(("sec", "tile")),
        P(),
        P(),
        P(("sec", "tile"), None),
        P(("sec", "tile"), None, None),
        P(None, None, ("sec", "tile")),
        P(None, None, ("sec", "tile")),
        P(None, ("sec", "tile")),
        P(),
    )
    out_specs = (P(None, ("sec", "tile"), None), P(None, None, ("sec", "tile")))
    return jax.shard_map(
        on_device, mesh=mesh, in_specs=in_specs, out_specs=out_specs, check_vma=False
    )
```

```python
import jax
import jax.numpy as jnp
from jax import lax
from jax.experimental import pallas as pl
from jax.experimental.pallas import tpu as pltpu
from jax.sharding import PartitionSpec as P


def threshold_table(count):
    diameter = 4e-05 * jnp.power(jnp.float32(1.35), jnp.arange(count).astype(jnp.float32))
    return jnp.sqrt(0.0123 * (2160.0 * 9.81 * diameter + 0.0003 / (1.227 * diameter)))


def emit(wind_rows, moist_rows, texture_rows, erodible, mass_frac, blast_table, base_thresh):
    high = lax.Precision.HIGHEST
    thresh = base_thresh[:, None, None] * jnp.sqrt(1.0 + 12.1 * moist_rows)[None]
    classes = jnp.arange(mass_frac.shape[0])
    onehot = (texture_rows[None] == classes[:, None, None]).astype(jnp.float32)
    fraction = jnp.einsum("tb,tnl->bnl", mass_frac, onehot, precision=high)
    speed = wind_rows[None]
    salt = (
        40.0
        * fraction
        * erodible[None]
        * (speed + thresh)
        * jnp.maximum(speed * speed - thresh * thresh, 0.0)
    )
    blasted = jnp.einsum("tkb,bnl->tknl", blast_table, salt, precision=high)
    emission = jnp.sum(blasted * onehot[:, None], axis=0)
    return jnp.transpose(emission, (1, 0, 2)).astype(jnp.bfloat16)


def lookup_kernel(index_ref, parts_ref, out_ref):
    rows_per_step, lanes = index_ref.shape
    segments = parts_ref.shape[1] // 3
    levels = lax.broadcasted_iota(jnp.int32, (segments, lanes), 0).astype(jnp.bfloat16)
    lane_rows = lax.broadcasted_iota(jnp.int32, (128, lanes), 0)
    one = jnp.ones((segments, lanes), jnp.bfloat16)
    zero = jnp.zeros((segments, lanes), jnp.bfloat16)
    for r in range(rows_per_step):
        cell = index_ref[r : r + 1, :]
        high_part = (cell // 128).astype(jnp.bfloat16)
        low_part = cell % 128
        pick_row = jnp.where(levels == high_part, one, zero)
        stacked = jnp.concatenate([pick_row, pick_row, pick_row], axis=0)
        row_values = jnp.dot(parts_ref[...], stacked, preferred_element_type=jnp.float32)
        pick_lane = lane_rows == low_part
        out_ref[r : r + 1, :] = jnp.sum(jnp.where(pick_lane, row_values, 0.0), axis=0, keepdims=True)


def lookup(table, index):
    segments = table.shape[0] // 128
    grid = table.reshape(segments, 128)
    first_wide = lax.reduce_precision(grid, exponent_bits=8, mantissa_bits=7)
    rest = grid - first_wide
    second_wide = lax.reduce_precision(rest, exponent_bits=8, mantissa_bits=7)
    parts = jnp.concatenate([first_wide, second_wide, rest - second_wide], axis=0).T.astype(jnp.bfloat16)
    rows, lanes = index.shape
    step = 8
    return pl.pallas_call(
        lookup_kernel,
        out_shape=jax.ShapeDtypeStruct((rows, lanes), jnp.float32),
        grid=(rows // step,),
        in_specs=[
            pl.BlockSpec((step, lanes), lambda i: (i, 0)),
            pl.BlockSpec((128, 3 * segments), lambda i: (0, 0)),
        ],
        out_specs=pl.BlockSpec((step, lanes), lambda i: (i, 0)),
        compiler_params=pltpu.CompilerParams(vmem_limit_bytes=8 * 1024 * 1024),
        cost_estimate=pl.CostEstimate(
            flops=2 * 384 * segments * rows * lanes, transcendentals=0,
            bytes_accessed=8 * rows * lanes + 768 * segments,
        ),
    )(index, parts)

def solve(right_side, coupling, sinking):
    levels = right_side.shape[1]
    sink_col = sinking[:, None]
    zero_row = jnp.zeros_like(coupling[0])
    ratios = []
    partial_value = []
    ratio_prev = None
    part_prev = None
    for level in range(levels):
        lower_c = coupling[level - 1] if level > 0 else zero_row
        upper_c = coupling[level] if level < levels - 1 else zero_row
        diagonal = 1.0 + lower_c[None] + upper_c[None] + sink_col
        if level == 0:
            pivot = diagonal
            part_now = right_side[:, level] / pivot
        else:
            pivot = diagonal + lower_c[None] * ratio_prev
            part_now = (right_side[:, level] + lower_c[None] * part_prev) / pivot
        if level < levels - 1:
            ratio_now = -(upper_c[None] + sink_col) / pivot
        else:
            ratio_now = jnp.zeros_like(pivot)
        ratios.append(ratio_now)
        partial_value.append(part_now)
        ratio_prev = ratio_now
        part_prev = part_now
    result = [None] * levels
    result[levels - 1] = partial_value[levels - 1]
    for level in range(levels - 2, -1, -1):
        result[level] = partial_value[level] - ratios[level] * result[level + 1]
    return jnp.stack(result, axis=1)


def surface_kernel(state_ref, coupling_ref, out_ref):
    fields, levels, columns = state_ref.shape
    zero_row = jnp.zeros((1, columns), jnp.float32)
    ratios = []
    partial_value = [[] for _ in range(fields)]
    ratio_prev = None
    for level in range(levels):
        lower_c = coupling_ref[level - 1 : level, :] if level > 0 else zero_row
        upper_c = coupling_ref[level : level + 1, :] if level < levels - 1 else zero_row
        diagonal = 1.0 + lower_c + upper_c
        pivot = diagonal if level == 0 else diagonal + lower_c * ratio_prev
        for f in range(fields):
            rhs = state_ref[f, level : level + 1, :]
            if level == 0:
                partial_value[f].append(rhs / pivot)
            else:
                partial_value[f].append((rhs + lower_c * partial_value[f][-1]) / pivot)
        ratio_now = -upper_c / pivot if level < levels - 1 else zero_row
        ratios.append(ratio_now)
        ratio_prev = ratio_now
    lowest = []
    for f in range(fields):
        result = partial_value[f][levels - 1]
        for level in range(levels - 2, -1, -1):
            result = partial_value[f][level] - ratios[level] * result
        lowest.append(result)
    out_ref[0:1, :] = jnp.sqrt(lowest[0] * lowest[0] + lowest[1] * lowest[1] + 0.25)
    out_ref[1:2, :] = lowest[2]


def surface_of(atm_state, mixing):
    columns = atm_state.shape[2]
    return pl.pallas_call(
        surface_kernel,
        out_shape=jax.ShapeDtypeStruct((2, columns), jnp.float32),
        compiler_params=pltpu.CompilerParams(vmem_limit_bytes=8 * 1024 * 1024),
    )(atm_state, mixing)


def on_device(
    land_wind,
    land_moist,
    texture,
    land_index,
    erod_map,
    mass_frac,
    blast_table,
    dest_tile,
    regrid_w,
    atm_state,
    dust_mix,
    mixing,
    settle,
):
    high = lax.Precision.HIGHEST
    nblocks, ncells = land_wind.shape
    columns = atm_state.shape[2]
    nbins = blast_table.shape[1]
    devices = lax.axis_size(("sec", "tile"))
    surface = surface_of(atm_state, mixing).astype(jnp.bfloat16).reshape(1, 2 * columns)
    base_thresh = threshold_table(mass_frac.shape[1])
    erodible = lookup(erod_map, land_index)
    emission = emit(land_wind, land_moist, texture, erodible, mass_frac, blast_table, base_thresh)
    partial_flux = jnp.einsum(
        "gkl,gla->gka", emission, regrid_w, preferred_element_type=jnp.float32
    )
    flat_flux = partial_flux.reshape(nblocks, nbins * columns)
    targets = dest_tile[:, 0]
    onehot = (targets[:, None] == jnp.arange(devices)[None, :]).astype(jnp.float32)
    dims = (((0,), (0,)), ((), ()))
    outgoing = lax.dot_general(onehot, flat_flux, dims, precision=high)
    spread = jnp.broadcast_to(surface, (devices, 2 * columns))
    half = nbins * columns // 2
    payload = jnp.concatenate(
        [outgoing.astype(jnp.bfloat16).reshape(devices, 2, half), spread.reshape(devices, 2, columns)], axis=2
    )
    incoming = lax.all_to_all(payload, ("sec", "tile"), split_axis=0, concat_axis=0, tiled=True)
    flux = jnp.sum(incoming[:, :, :half].astype(jnp.float32), axis=0).reshape(nbins, columns)
    gathered = incoming[:, :, half:].reshape(devices, 2 * columns)
    flux = flux * (float(columns) / float(ncells * nblocks))
    loaded = dust_mix.at[:, 0, :].add(flux)
    dust_out = solve(loaded, mixing, settle)
    picked = jnp.dot(onehot.astype(jnp.bfloat16), gathered, preferred_element_type=jnp.float32)
    picked = picked.astype(jnp.bfloat16).reshape(nblocks, 2, columns)
    picked = jnp.concatenate([picked, jnp.ones((nblocks, 1, columns), jnp.bfloat16)], axis=1)
    numer = jnp.einsum("gla,gka->kgl", regrid_w, picked, preferred_element_type=jnp.float32)
    denom = numer[2]
    land_fields = jnp.stack([numer[0] / denom, 0.5 * land_moist + 0.5 * numer[1] / denom])
    return (land_fields, dust_out)


def solution(mesh):
    in_specs = (
        P(("sec", "tile"), None),
        P(("sec", "tile"), None),
        P(("sec", "tile"), None),
        P(("sec", "tile"), None),
        P(("sec", "tile")),
        P(),
        P(),
        P(("sec", "tile"), None),
        P(("sec", "tile"), None, None),
        P(None, None, ("sec", "tile")),
        P(None, None, ("sec", "tile")),
        P(None, ("sec", "tile")),
        P(),
    )
    out_specs = (P(None, ("sec", "tile"), None), P(None, None, ("sec", "tile")))
    return jax.shard_map(
        on_device, mesh=mesh, in_specs=in_specs, out_specs=out_specs, check_vma=False
    )
```

```python
import jax
import jax.numpy as jnp
from jax import lax
from jax.experimental import pallas as pl
from jax.experimental.pallas import tpu as pltpu
from jax.sharding import PartitionSpec as P


def threshold_table(count):
    diameter = 4e-05 * jnp.power(jnp.float32(1.35), jnp.arange(count).astype(jnp.float32))
    return jnp.sqrt(0.0123 * (2160.0 * 9.81 * diameter + 0.0003 / (1.227 * diameter)))


def emit(wind_rows, moist_rows, texture_rows, erodible, mass_frac, blast_table, base_thresh):
    high = lax.Precision.HIGHEST
    thresh = base_thresh[:, None, None] * jnp.sqrt(1.0 + 12.1 * moist_rows)[None]
    classes = jnp.arange(mass_frac.shape[0])
    onehot = (texture_rows[None] == classes[:, None, None]).astype(jnp.float32)
    fraction = jnp.zeros((mass_frac.shape[1],) + texture_rows.shape, jnp.float32)
    for t in range(mass_frac.shape[0]):
        fraction = jnp.where(texture_rows[None] == t, mass_frac[t][:, None, None], fraction)
    speed = wind_rows[None]
    salt = (
        40.0
        * fraction
        * erodible[None]
        * (speed + thresh)
        * jnp.maximum(speed * speed - thresh * thresh, 0.0)
    )
    blasted = jnp.einsum("tkb,bnl->tknl", blast_table, salt, precision=high)
    emission = jnp.sum(blasted * onehot[:, None], axis=0)
    return jnp.transpose(emission, (1, 0, 2)).astype(jnp.bfloat16)


def lookup_kernel(index_ref, table_ref, out_ref, parts_ref):
    rows_per_step, lanes = index_ref.shape
    segments = table_ref.shape[0]

    @pl.when(pl.program_id(0) == 0)
    def _():
        grid = table_ref[...]
        first = grid.astype(jnp.bfloat16)
        rest = grid - first.astype(jnp.float32)
        second = rest.astype(jnp.bfloat16)
        third = rest - second.astype(jnp.float32)
        for p, part in enumerate((first.astype(jnp.float32), second.astype(jnp.float32), third)):
            parts_ref[:, p * segments : (p + 1) * segments] = part.T.astype(jnp.bfloat16)

    levels = lax.broadcasted_iota(jnp.int32, (segments, lanes), 0).astype(jnp.bfloat16)
    lane_rows = lax.broadcasted_iota(jnp.int32, (128, lanes), 0)
    one = jnp.ones((segments, lanes), jnp.bfloat16)
    zero = jnp.zeros((segments, lanes), jnp.bfloat16)
    for r in range(rows_per_step):
        cell = index_ref[r : r + 1, :]
        high_part = (cell // 128).astype(jnp.bfloat16)
        low_part = cell % 128
        pick_row = jnp.where(levels == high_part, one, zero)
        stacked = jnp.concatenate([pick_row, pick_row, pick_row], axis=0)
        row_values = jnp.dot(parts_ref[...], stacked, preferred_element_type=jnp.float32)
        pick_lane = lane_rows == low_part
        out_ref[r : r + 1, :] = jnp.sum(jnp.where(pick_lane, row_values, 0.0), axis=0, keepdims=True)


def lookup(table, index):
    segments = table.shape[0] // 128
    rows, lanes = index.shape
    step = 8
    return pl.pallas_call(
        lookup_kernel,
        out_shape=jax.ShapeDtypeStruct((rows, lanes), jnp.float32),
        grid=(rows // step,),
        in_specs=[
            pl.BlockSpec((step, lanes), lambda i: (i, 0)),
            pl.BlockSpec((segments, 128), lambda i: (0, 0)),
        ],
        out_specs=pl.BlockSpec((step, lanes), lambda i: (i, 0)),
        scratch_shapes=[pltpu.VMEM((128, 3 * segments), jnp.bfloat16)],
        compiler_params=pltpu.CompilerParams(vmem_limit_bytes=8 * 1024 * 1024),
        cost_estimate=pl.CostEstimate(
            flops=2 * 384 * segments * rows * lanes, transcendentals=0,
            bytes_accessed=8 * rows * lanes + 512 * segments,
        ),
    )(index, table.reshape(segments, 128))

def solve(right_side, coupling, sinking):
    levels = right_side.shape[1]
    sink_col = sinking[:, None]
    zero_row = jnp.zeros_like(coupling[0])
    ratios = []
    partial_value = []
    ratio_prev = None
    part_prev = None
    for level in range(levels):
        lower_c = coupling[level - 1] if level > 0 else zero_row
        upper_c = coupling[level] if level < levels - 1 else zero_row
        diagonal = 1.0 + lower_c[None] + upper_c[None] + sink_col
        if level == 0:
            pivot = diagonal
            part_now = right_side[:, level] / pivot
        else:
            pivot = diagonal + lower_c[None] * ratio_prev
            part_now = (right_side[:, level] + lower_c[None] * part_prev) / pivot
        if level < levels - 1:
            ratio_now = -(upper_c[None] + sink_col) / pivot
        else:
            ratio_now = jnp.zeros_like(pivot)
        ratios.append(ratio_now)
        partial_value.append(part_now)
        ratio_prev = ratio_now
        part_prev = part_now
    result = [None] * levels
    result[levels - 1] = partial_value[levels - 1]
    for level in range(levels - 2, -1, -1):
        result[level] = partial_value[level] - ratios[level] * result[level + 1]
    return jnp.stack(result, axis=1)


def surface_kernel(state_ref, coupling_ref, out_ref):
    fields, levels, columns = state_ref.shape
    zero_row = jnp.zeros((1, columns), jnp.float32)
    ratios = []
    partial_value = [[] for _ in range(fields)]
    ratio_prev = None
    for level in range(levels):
        lower_c = coupling_ref[level - 1 : level, :] if level > 0 else zero_row
        upper_c = coupling_ref[level : level + 1, :] if level < levels - 1 else zero_row
        diagonal = 1.0 + lower_c + upper_c
        pivot = diagonal if level == 0 else diagonal + lower_c * ratio_prev
        for f in range(fields):
            rhs = state_ref[f, level : level + 1, :]
            if level == 0:
                partial_value[f].append(rhs / pivot)
            else:
                partial_value[f].append((rhs + lower_c * partial_value[f][-1]) / pivot)
        ratio_now = -upper_c / pivot if level < levels - 1 else zero_row
        ratios.append(ratio_now)
        ratio_prev = ratio_now
    lowest = []
    for f in range(fields):
        result = partial_value[f][levels - 1]
        for level in range(levels - 2, -1, -1):
            result = partial_value[f][level] - ratios[level] * result
        lowest.append(result)
    out_ref[0:1, :] = jnp.sqrt(lowest[0] * lowest[0] + lowest[1] * lowest[1] + 0.25)
    out_ref[1:2, :] = lowest[2]


def surface_of(atm_state, mixing):
    columns = atm_state.shape[2]
    return pl.pallas_call(
        surface_kernel,
        out_shape=jax.ShapeDtypeStruct((2, columns), jnp.float32),
        compiler_params=pltpu.CompilerParams(vmem_limit_bytes=8 * 1024 * 1024),
    )(atm_state, mixing)


def on_device(
    land_wind,
    land_moist,
    texture,
    land_index,
    erod_map,
    mass_frac,
    blast_table,
    dest_tile,
    regrid_w,
    atm_state,
    dust_mix,
    mixing,
    settle,
):
    high = lax.Precision.HIGHEST
    nblocks, ncells = land_wind.shape
    columns = atm_state.shape[2]
    nbins = blast_table.shape[1]
    devices = lax.axis_size(("sec", "tile"))
    surface = surface_of(atm_state, mixing).astype(jnp.bfloat16).reshape(1, 2 * columns)
    base_thresh = threshold_table(mass_frac.shape[1])
    erodible = lookup(erod_map, land_index)
    emission = emit(land_wind, land_moist, texture, erodible, mass_frac, blast_table, base_thresh)
    partial_flux = jnp.einsum(
        "gkl,gla->gka", emission, regrid_w, preferred_element_type=jnp.float32
    )
    flat_flux = partial_flux.reshape(nblocks, nbins * columns)
    targets = dest_tile[:, 0]
    onehot = (targets[:, None] == jnp.arange(devices)[None, :]).astype(jnp.float32)
    dims = (((0,), (0,)), ((), ()))
    outgoing = lax.dot_general(onehot, flat_flux, dims, precision=high)
    spread = jnp.broadcast_to(surface, (devices, 2 * columns))
    half = nbins * columns // 2
    payload = jnp.concatenate(
        [outgoing.astype(jnp.bfloat16).reshape(devices, 2, half), spread.reshape(devices, 2, columns)], axis=2
    )
    incoming = lax.all_to_all(payload, ("sec", "tile"), split_axis=0, concat_axis=0, tiled=True)
    flux = jnp.sum(incoming[:, :, :half].astype(jnp.float32), axis=0).reshape(nbins, columns)
    gathered = incoming[:, :, half:].reshape(devices, 2 * columns)
    flux = flux * (float(columns) / float(ncells * nblocks))
    loaded = dust_mix.at[:, 0, :].add(flux)
    dust_out = solve(loaded, mixing, settle)
    picked = jnp.dot(onehot.astype(jnp.bfloat16), gathered, preferred_element_type=jnp.float32)
    picked = picked.astype(jnp.bfloat16).reshape(nblocks, 2, columns)
    picked = jnp.concatenate([picked, jnp.ones((nblocks, 1, columns), jnp.bfloat16)], axis=1)
    numer = jnp.einsum("gla,gka->kgl", regrid_w, picked, preferred_element_type=jnp.float32)
    denom = numer[2]
    land_fields = jnp.stack([numer[0] / denom, 0.5 * land_moist + 0.5 * numer[1] / denom])
    return (land_fields, dust_out)


def solution(mesh):
    in_specs = (
        P(("sec", "tile"), None),
        P(("sec", "tile"), None),
        P(("sec", "tile"), None),
        P(("sec", "tile"), None),
        P(("sec", "tile")),
        P(),
        P(),
        P(("sec", "tile"), None),
        P(("sec", "tile"), None, None),
        P(None, None, ("sec", "tile")),
        P(None, None, ("sec", "tile")),
        P(None, ("sec", "tile")),
        P(),
    )
    out_specs = (P(None, ("sec", "tile"), None), P(None, None, ("sec", "tile")))
    return jax.shard_map(
        on_device, mesh=mesh, in_specs=in_specs, out_specs=out_specs, check_vma=False
    )
```

```python
import jax
import jax.numpy as jnp
from jax import lax
from jax.experimental import pallas as pl
from jax.experimental.pallas import tpu as pltpu
from jax.sharding import PartitionSpec as P


def threshold_table(count):
    diameter = 4e-05 * jnp.power(jnp.float32(1.35), jnp.arange(count).astype(jnp.float32))
    return jnp.sqrt(0.0123 * (2160.0 * 9.81 * diameter + 0.0003 / (1.227 * diameter)))


def emit(wind_rows, moist_rows, texture_rows, erodible, mass_frac, blast_table, base_thresh):
    high = lax.Precision.HIGHEST
    thresh = base_thresh[:, None, None] * jnp.sqrt(1.0 + 12.1 * moist_rows)[None]
    classes = jnp.arange(mass_frac.shape[0])
    onehot = (texture_rows[None] == classes[:, None, None]).astype(jnp.float32)
    fraction = jnp.einsum("tb,tnl->bnl", mass_frac, onehot, precision=high)
    speed = wind_rows[None]
    salt = (
        40.0
        * fraction
        * erodible[None]
        * (speed + thresh)
        * jnp.maximum(speed * speed - thresh * thresh, 0.0)
    )
    blasted = jnp.einsum("tkb,bnl->tknl", blast_table, salt, precision=high)
    emission = jnp.sum(blasted * onehot[:, None], axis=0)
    return jnp.transpose(emission, (1, 0, 2)).astype(jnp.bfloat16)


def lookup_kernel(index_ref, table_ref, out_ref, parts_ref):
    rows_per_step, lanes = index_ref.shape
    segments = table_ref.shape[0]

    @pl.when(pl.program_id(0) == 0)
    def _():
        grid = table_ref[...]
        first = grid.astype(jnp.bfloat16)
        rest = grid - first.astype(jnp.float32)
        second = rest.astype(jnp.bfloat16)
        third = rest - second.astype(jnp.float32)
        for p, part in enumerate((first.astype(jnp.float32), second.astype(jnp.float32), third)):
            parts_ref[:, p * segments : (p + 1) * segments] = part.T.astype(jnp.bfloat16)

    levels = lax.broadcasted_iota(jnp.int32, (segments, lanes), 0).astype(jnp.bfloat16)
    lane_rows = lax.broadcasted_iota(jnp.int32, (128, lanes), 0)
    one = jnp.ones((segments, lanes), jnp.bfloat16)
    zero = jnp.zeros((segments, lanes), jnp.bfloat16)
    for r in range(rows_per_step):
        cell = index_ref[r : r + 1, :]
        high_part = (cell // 128).astype(jnp.bfloat16)
        low_part = cell % 128
        pick_row = jnp.where(levels == high_part, one, zero)
        stacked = jnp.concatenate([pick_row, pick_row, pick_row], axis=0)
        row_values = jnp.dot(parts_ref[...], stacked, preferred_element_type=jnp.float32)
        pick_lane = lane_rows == low_part
        out_ref[r : r + 1, :] = jnp.sum(jnp.where(pick_lane, row_values, 0.0), axis=0, keepdims=True)


def lookup(table, index):
    segments = table.shape[0] // 128
    rows, lanes = index.shape
    step = 8
    return pl.pallas_call(
        lookup_kernel,
        out_shape=jax.ShapeDtypeStruct((rows, lanes), jnp.float32),
        grid=(rows // step,),
        in_specs=[
            pl.BlockSpec((step, lanes), lambda i: (i, 0)),
            pl.BlockSpec((segments, 128), lambda i: (0, 0)),
        ],
        out_specs=pl.BlockSpec((step, lanes), lambda i: (i, 0)),
        scratch_shapes=[pltpu.VMEM((128, 3 * segments), jnp.bfloat16)],
        compiler_params=pltpu.CompilerParams(vmem_limit_bytes=8 * 1024 * 1024),
        cost_estimate=pl.CostEstimate(
            flops=2 * 384 * segments * rows * lanes, transcendentals=0,
            bytes_accessed=8 * rows * lanes + 512 * segments,
        ),
    )(index, table.reshape(segments, 128))

def solve(right_side, coupling, sinking):
    levels = right_side.shape[1]
    sink_col = sinking[:, None]
    zero_row = jnp.zeros_like(coupling[0])
    ratios = []
    partial_value = []
    ratio_prev = None
    part_prev = None
    for level in range(levels):
        lower_c = coupling[level - 1] if level > 0 else zero_row
        upper_c = coupling[level] if level < levels - 1 else zero_row
        diagonal = 1.0 + lower_c[None] + upper_c[None] + sink_col
        if level == 0:
            pivot = diagonal
            part_now = right_side[:, level] / pivot
        else:
            pivot = diagonal + lower_c[None] * ratio_prev
            part_now = (right_side[:, level] + lower_c[None] * part_prev) / pivot
        if level < levels - 1:
            ratio_now = -(upper_c[None] + sink_col) / pivot
        else:
            ratio_now = jnp.zeros_like(pivot)
        ratios.append(ratio_now)
        partial_value.append(part_now)
        ratio_prev = ratio_now
        part_prev = part_now
    result = [None] * levels
    result[levels - 1] = partial_value[levels - 1]
    for level in range(levels - 2, -1, -1):
        result[level] = partial_value[level] - ratios[level] * result[level + 1]
    return jnp.stack(result, axis=1)


def surface_kernel(state_ref, coupling_ref, out_ref):
    fields, levels, columns = state_ref.shape
    zero_row = jnp.zeros((1, columns), jnp.float32)
    ratios = []
    partial_value = [[] for _ in range(fields)]
    ratio_prev = None
    for level in range(levels):
        lower_c = coupling_ref[level - 1 : level, :] if level > 0 else zero_row
        upper_c = coupling_ref[level : level + 1, :] if level < levels - 1 else zero_row
        diagonal = 1.0 + lower_c + upper_c
        pivot = diagonal if level == 0 else diagonal + lower_c * ratio_prev
        for f in range(fields):
            rhs = state_ref[f, level : level + 1, :]
            if level == 0:
                partial_value[f].append(rhs / pivot)
            else:
                partial_value[f].append((rhs + lower_c * partial_value[f][-1]) / pivot)
        ratio_now = -upper_c / pivot if level < levels - 1 else zero_row
        ratios.append(ratio_now)
        ratio_prev = ratio_now
    lowest = []
    for f in range(fields):
        result = partial_value[f][levels - 1]
        for level in range(levels - 2, -1, -1):
            result = partial_value[f][level] - ratios[level] * result
        lowest.append(result)
    out_ref[0:1, :] = jnp.sqrt(lowest[0] * lowest[0] + lowest[1] * lowest[1] + 0.25)
    out_ref[1:2, :] = lowest[2]


def surface_of(atm_state, mixing):
    columns = atm_state.shape[2]
    return pl.pallas_call(
        surface_kernel,
        out_shape=jax.ShapeDtypeStruct((2, columns), jnp.float32),
        compiler_params=pltpu.CompilerParams(vmem_limit_bytes=8 * 1024 * 1024),
    )(atm_state, mixing)


def on_device(
    land_wind,
    land_moist,
    texture,
    land_index,
    erod_map,
    mass_frac,
    blast_table,
    dest_tile,
    regrid_w,
    atm_state,
    dust_mix,
    mixing,
    settle,
):
    high = lax.Precision.HIGHEST
    nblocks, ncells = land_wind.shape
    columns = atm_state.shape[2]
    nbins = blast_table.shape[1]
    devices = lax.axis_size(("sec", "tile"))
    surface = surface_of(atm_state, mixing).astype(jnp.bfloat16).reshape(1, 2 * columns)
    base_thresh = threshold_table(mass_frac.shape[1])
    erodible = lookup(erod_map, land_index)
    emission = emit(land_wind, land_moist, texture, erodible, mass_frac, blast_table, base_thresh)
    partial_flux = jnp.einsum(
        "gkl,gla->gka", emission, regrid_w, preferred_element_type=jnp.float32
    )
    flat_flux = partial_flux.reshape(nblocks, nbins * columns)
    targets = dest_tile[:, 0]
    onehot = (targets[:, None] == jnp.arange(devices)[None, :]).astype(jnp.float32)
    dims = (((0,), (0,)), ((), ()))
    outgoing = lax.dot_general(onehot, flat_flux, dims, precision=high)
    spread = jnp.broadcast_to(surface, (devices, 2 * columns))
    half = nbins * columns // 2
    payload = jnp.concatenate(
        [outgoing.astype(jnp.bfloat16).reshape(devices, 2, half), spread.reshape(devices, 2, columns)], axis=2
    )
    incoming = lax.all_to_all(payload, ("sec", "tile"), split_axis=0, concat_axis=0, tiled=True)
    flux = jnp.sum(incoming[:, :, :half].astype(jnp.float32), axis=0).reshape(nbins, columns)
    gathered = incoming[:, :, half:].reshape(devices, 2 * columns)
    flux = flux * (float(columns) / float(ncells * nblocks))
    loaded = dust_mix.at[:, 0, :].add(flux)
    dust_out = solve(loaded, mixing, settle)
    picked = jnp.dot(onehot.astype(jnp.bfloat16), gathered, preferred_element_type=jnp.float32)
    picked = picked.astype(jnp.bfloat16).reshape(nblocks, 2, columns)
    picked = jnp.concatenate([picked, jnp.ones((nblocks, 1, columns), jnp.bfloat16)], axis=1)
    numer = jnp.einsum("gla,gka->kgl", regrid_w, picked, preferred_element_type=jnp.float32)
    denom = numer[2]
    land_fields = jnp.stack([numer[0] / denom, 0.5 * land_moist + 0.5 * numer[1] / denom])
    return (land_fields, dust_out)


def solution(mesh):
    in_specs = (
        P(("sec", "tile"), None),
        P(("sec", "tile"), None),
        P(("sec", "tile"), None),
        P(("sec", "tile"), None),
        P(("sec", "tile")),
        P(),
        P(),
        P(("sec", "tile"), None),
        P(("sec", "tile"), None, None),
        P(None, None, ("sec", "tile")),
        P(None, None, ("sec", "tile")),
        P(None, ("sec", "tile")),
        P(),
    )
    out_specs = (P(None, ("sec", "tile"), None), P(None, None, ("sec", "tile")))
    return jax.shard_map(
        on_device, mesh=mesh, in_specs=in_specs, out_specs=out_specs, check_vma=False
    )
```

```python
import jax
import jax.numpy as jnp
from jax import lax
from jax.experimental import pallas as pl
from jax.experimental.pallas import tpu as pltpu
from jax.sharding import PartitionSpec as P


def threshold_table(count):
    diameter = 4e-05 * jnp.power(jnp.float32(1.35), jnp.arange(count).astype(jnp.float32))
    return jnp.sqrt(0.0123 * (2160.0 * 9.81 * diameter + 0.0003 / (1.227 * diameter)))


def emit(wind_rows, moist_rows, texture_rows, erodible, mass_frac, blast_table, base_thresh):
    high = lax.Precision.HIGHEST
    thresh = base_thresh[:, None, None] * jnp.sqrt(1.0 + 12.1 * moist_rows)[None]
    classes = jnp.arange(mass_frac.shape[0])
    onehot = (texture_rows[None] == classes[:, None, None]).astype(jnp.float32)
    fraction = jnp.einsum("tb,tnl->bnl", mass_frac, onehot, precision=high)
    speed = wind_rows[None]
    salt = (
        40.0
        * fraction
        * erodible[None]
        * (speed + thresh)
        * jnp.maximum(speed * speed - thresh * thresh, 0.0)
    )
    blasted = jnp.einsum("tkb,bnl->tknl", blast_table, salt, precision=high)
    emission = jnp.sum(blasted * onehot[:, None], axis=0)
    return jnp.transpose(emission, (1, 0, 2)).astype(jnp.bfloat16)


def lookup_kernel(index_ref, parts_ref, out_ref):
    rows_per_step, lanes = index_ref.shape
    segments = parts_ref.shape[1] // 3
    levels = lax.broadcasted_iota(jnp.int32, (segments, lanes), 0).astype(jnp.bfloat16)
    lane_rows = lax.broadcasted_iota(jnp.int32, (128, lanes), 0)
    one = jnp.ones((segments, lanes), jnp.bfloat16)
    zero = jnp.zeros((segments, lanes), jnp.bfloat16)
    for r in range(rows_per_step):
        cell = index_ref[r : r + 1, :]
        high_part = (cell // 128).astype(jnp.bfloat16)
        low_part = cell % 128
        pick_row = jnp.where(levels == high_part, one, zero)
        stacked = jnp.concatenate([pick_row, pick_row, pick_row], axis=0)
        row_values = jnp.dot(parts_ref[...], stacked, preferred_element_type=jnp.float32)
        pick_lane = lane_rows == low_part
        out_ref[r : r + 1, :] = jnp.sum(jnp.where(pick_lane, row_values, 0.0), axis=0, keepdims=True)


def lookup(table, index):
    segments = table.shape[0] // 128
    grid = table.reshape(segments, 128)
    first_wide = lax.reduce_precision(grid, exponent_bits=8, mantissa_bits=7)
    rest = grid - first_wide
    second_wide = lax.reduce_precision(rest, exponent_bits=8, mantissa_bits=7)
    parts = jnp.concatenate([first_wide, second_wide, rest - second_wide], axis=0).T.astype(jnp.bfloat16)
    rows, lanes = index.shape
    step = 32
    return pl.pallas_call(
        lookup_kernel,
        out_shape=jax.ShapeDtypeStruct((rows, lanes), jnp.float32),
        grid=(rows // step,),
        in_specs=[
            pl.BlockSpec((step, lanes), lambda i: (i, 0)),
            pl.BlockSpec((128, 3 * segments), lambda i: (0, 0)),
        ],
        out_specs=pl.BlockSpec((step, lanes), lambda i: (i, 0)),
        compiler_params=pltpu.CompilerParams(vmem_limit_bytes=8 * 1024 * 1024),
        cost_estimate=pl.CostEstimate(
            flops=2 * 384 * segments * rows * lanes, transcendentals=0,
            bytes_accessed=8 * rows * lanes + 768 * segments,
        ),
    )(index, parts)

def solve(right_side, coupling, sinking):
    levels = right_side.shape[1]
    sink_col = sinking[:, None]
    zero_row = jnp.zeros_like(coupling[0])
    ratios = []
    partial_value = []
    ratio_prev = None
    part_prev = None
    for level in range(levels):
        lower_c = coupling[level - 1] if level > 0 else zero_row
        upper_c = coupling[level] if level < levels - 1 else zero_row
        diagonal = 1.0 + lower_c[None] + upper_c[None] + sink_col
        if level == 0:
            pivot = diagonal
            part_now = right_side[:, level] / pivot
        else:
            pivot = diagonal + lower_c[None] * ratio_prev
            part_now = (right_side[:, level] + lower_c[None] * part_prev) / pivot
        if level < levels - 1:
            ratio_now = -(upper_c[None] + sink_col) / pivot
        else:
            ratio_now = jnp.zeros_like(pivot)
        ratios.append(ratio_now)
        partial_value.append(part_now)
        ratio_prev = ratio_now
        part_prev = part_now
    result = [None] * levels
    result[levels - 1] = partial_value[levels - 1]
    for level in range(levels - 2, -1, -1):
        result[level] = partial_value[level] - ratios[level] * result[level + 1]
    return jnp.stack(result, axis=1)


def surface_kernel(state_ref, coupling_ref, out_ref):
    fields, levels, columns = state_ref.shape
    zero_row = jnp.zeros((1, columns), jnp.float32)
    ratios = []
    partial_value = [[] for _ in range(fields)]
    ratio_prev = None
    for level in range(levels):
        lower_c = coupling_ref[level - 1 : level, :] if level > 0 else zero_row
        upper_c = coupling_ref[level : level + 1, :] if level < levels - 1 else zero_row
        diagonal = 1.0 + lower_c + upper_c
        pivot = diagonal if level == 0 else diagonal + lower_c * ratio_prev
        for f in range(fields):
            rhs = state_ref[f, level : level + 1, :]
            if level == 0:
                partial_value[f].append(rhs / pivot)
            else:
                partial_value[f].append((rhs + lower_c * partial_value[f][-1]) / pivot)
        ratio_now = -upper_c / pivot if level < levels - 1 else zero_row
        ratios.append(ratio_now)
        ratio_prev = ratio_now
    lowest = []
    for f in range(fields):
        result = partial_value[f][levels - 1]
        for level in range(levels - 2, -1, -1):
            result = partial_value[f][level] - ratios[level] * result
        lowest.append(result)
    out_ref[0:1, :] = jnp.sqrt(lowest[0] * lowest[0] + lowest[1] * lowest[1] + 0.25)
    out_ref[1:2, :] = lowest[2]


def surface_of(atm_state, mixing):
    columns = atm_state.shape[2]
    return pl.pallas_call(
        surface_kernel,
        out_shape=jax.ShapeDtypeStruct((2, columns), jnp.float32),
        compiler_params=pltpu.CompilerParams(vmem_limit_bytes=8 * 1024 * 1024),
    )(atm_state, mixing)


def on_device(
    land_wind,
    land_moist,
    texture,
    land_index,
    erod_map,
    mass_frac,
    blast_table,
    dest_tile,
    regrid_w,
    atm_state,
    dust_mix,
    mixing,
    settle,
):
    high = lax.Precision.HIGHEST
    nblocks, ncells = land_wind.shape
    columns = atm_state.shape[2]
    nbins = blast_table.shape[1]
    devices = lax.axis_size(("sec", "tile"))
    surface = surface_of(atm_state, mixing).astype(jnp.bfloat16).reshape(1, 2 * columns)
    base_thresh = threshold_table(mass_frac.shape[1])
    erodible = lookup(erod_map, land_index)
    emission = emit(land_wind, land_moist, texture, erodible, mass_frac, blast_table, base_thresh)
    partial_flux = jnp.einsum(
        "gkl,gla->gka", emission, regrid_w, preferred_element_type=jnp.float32
    )
    flat_flux = partial_flux.reshape(nblocks, nbins * columns)
    targets = dest_tile[:, 0]
    onehot = (targets[:, None] == jnp.arange(devices)[None, :]).astype(jnp.float32)
    dims = (((0,), (0,)), ((), ()))
    outgoing = lax.dot_general(onehot, flat_flux, dims, precision=high)
    spread = jnp.broadcast_to(surface, (devices, 2 * columns))
    half = nbins * columns // 2
    payload = jnp.concatenate(
        [outgoing.astype(jnp.bfloat16).reshape(devices, 2, half), spread.reshape(devices, 2, columns)], axis=2
    )
    incoming = lax.all_to_all(payload, ("sec", "tile"), split_axis=0, concat_axis=0, tiled=True)
    flux = jnp.sum(incoming[:, :, :half].astype(jnp.float32), axis=0).reshape(nbins, columns)
    gathered = incoming[:, :, half:].reshape(devices, 2 * columns)
    flux = flux * (float(columns) / float(ncells * nblocks))
    loaded = dust_mix.at[:, 0, :].add(flux)
    dust_out = solve(loaded, mixing, settle)
    picked = jnp.dot(onehot.astype(jnp.bfloat16), gathered, preferred_element_type=jnp.float32)
    picked = picked.astype(jnp.bfloat16).reshape(nblocks, 2, columns)
    picked = jnp.concatenate([picked, jnp.ones((nblocks, 1, columns), jnp.bfloat16)], axis=1)
    numer = jnp.einsum("gla,gka->kgl", regrid_w, picked, preferred_element_type=jnp.float32)
    denom = numer[2]
    land_fields = jnp.stack([numer[0] / denom, 0.5 * land_moist + 0.5 * numer[1] / denom])
    return (land_fields, dust_out)


def solution(mesh):
    in_specs = (
        P(("sec", "tile"), None),
        P(("sec", "tile"), None),
        P(("sec", "tile"), None),
        P(("sec", "tile"), None),
        P(("sec", "tile")),
        P(),
        P(),
        P(("sec", "tile"), None),
        P(("sec", "tile"), None, None),
        P(None, None, ("sec", "tile")),
        P(None, None, ("sec", "tile")),
        P(None, ("sec", "tile")),
        P(),
    )
    out_specs = (P(None, ("sec", "tile"), None), P(None, None, ("sec", "tile")))
    return jax.shard_map(
        on_device, mesh=mesh, in_specs=in_specs, out_specs=out_specs, check_vma=False
    )
```

```python
import jax
import jax.numpy as jnp
from jax import lax
from jax.experimental import pallas as pl
from jax.experimental.pallas import tpu as pltpu
from jax.sharding import PartitionSpec as P


def threshold_table(count):
    diameter = 4e-05 * jnp.power(jnp.float32(1.35), jnp.arange(count).astype(jnp.float32))
    return jnp.sqrt(0.0123 * (2160.0 * 9.81 * diameter + 0.0003 / (1.227 * diameter)))


def emit(wind_rows, moist_rows, texture_rows, erodible, mass_frac, blast_table, base_thresh):
    high = lax.Precision.HIGHEST
    thresh = base_thresh[:, None, None] * jnp.sqrt(1.0 + 12.1 * moist_rows)[None]
    classes = jnp.arange(mass_frac.shape[0])
    onehot = (texture_rows[None] == classes[:, None, None]).astype(jnp.float32)
    fraction = jnp.einsum("tb,tnl->bnl", mass_frac, onehot, precision=high)
    speed = wind_rows[None]
    salt = (
        40.0
        * fraction
        * erodible[None]
        * (speed + thresh)
        * jnp.maximum(speed * speed - thresh * thresh, 0.0)
    )
    blasted = jnp.einsum("tkb,bnl->tknl", blast_table, salt, precision=high)
    emission = jnp.sum(blasted * onehot[:, None], axis=0)
    return jnp.transpose(emission, (1, 0, 2)).astype(jnp.bfloat16)


def lookup_kernel(index_ref, parts_ref, out_ref):
    rows_per_step, lanes = index_ref.shape
    segments = parts_ref.shape[1] // 3
    levels = lax.broadcasted_iota(jnp.int32, (segments, lanes), 0).astype(jnp.bfloat16)
    lane_rows = lax.broadcasted_iota(jnp.int32, (128, lanes), 0)
    one = jnp.ones((segments, lanes), jnp.bfloat16)
    zero = jnp.zeros((segments, lanes), jnp.bfloat16)
    for r in range(rows_per_step):
        cell = index_ref[r : r + 1, :]
        high_part = (cell // 128).astype(jnp.bfloat16)
        low_part = cell % 128
        pick_row = jnp.where(levels == high_part, one, zero)
        stacked = jnp.concatenate([pick_row, pick_row, pick_row], axis=0)
        row_values = jnp.dot(parts_ref[...], stacked, preferred_element_type=jnp.float32)
        pick_lane = lane_rows == low_part
        out_ref[r : r + 1, :] = jnp.sum(jnp.where(pick_lane, row_values, 0.0), axis=0, keepdims=True)


def lookup(table, index):
    segments = table.shape[0] // 128
    grid = table.reshape(segments, 128)
    first_wide = lax.reduce_precision(grid, exponent_bits=8, mantissa_bits=7)
    rest = grid - first_wide
    second_wide = lax.reduce_precision(rest, exponent_bits=8, mantissa_bits=7)
    parts = jnp.concatenate([first_wide, second_wide, rest - second_wide], axis=0).T.astype(jnp.bfloat16)
    rows, lanes = index.shape
    step = 128
    return pl.pallas_call(
        lookup_kernel,
        out_shape=jax.ShapeDtypeStruct((rows, lanes), jnp.float32),
        grid=(rows // step,),
        in_specs=[
            pl.BlockSpec((step, lanes), lambda i: (i, 0)),
            pl.BlockSpec((128, 3 * segments), lambda i: (0, 0)),
        ],
        out_specs=pl.BlockSpec((step, lanes), lambda i: (i, 0)),
        compiler_params=pltpu.CompilerParams(vmem_limit_bytes=8 * 1024 * 1024),
        cost_estimate=pl.CostEstimate(
            flops=2 * 384 * segments * rows * lanes, transcendentals=0,
            bytes_accessed=8 * rows * lanes + 768 * segments,
        ),
    )(index, parts)

def solve(right_side, coupling, sinking):
    levels = right_side.shape[1]
    sink_col = sinking[:, None]
    zero_row = jnp.zeros_like(coupling[0])
    ratios = []
    partial_value = []
    ratio_prev = None
    part_prev = None
    for level in range(levels):
        lower_c = coupling[level - 1] if level > 0 else zero_row
        upper_c = coupling[level] if level < levels - 1 else zero_row
        diagonal = 1.0 + lower_c[None] + upper_c[None] + sink_col
        if level == 0:
            pivot = diagonal
            part_now = right_side[:, level] / pivot
        else:
            pivot = diagonal + lower_c[None] * ratio_prev
            part_now = (right_side[:, level] + lower_c[None] * part_prev) / pivot
        if level < levels - 1:
            ratio_now = -(upper_c[None] + sink_col) / pivot
        else:
            ratio_now = jnp.zeros_like(pivot)
        ratios.append(ratio_now)
        partial_value.append(part_now)
        ratio_prev = ratio_now
        part_prev = part_now
    result = [None] * levels
    result[levels - 1] = partial_value[levels - 1]
    for level in range(levels - 2, -1, -1):
        result[level] = partial_value[level] - ratios[level] * result[level + 1]
    return jnp.stack(result, axis=1)


def surface_kernel(state_ref, coupling_ref, out_ref):
    fields, levels, columns = state_ref.shape
    zero_row = jnp.zeros((1, columns), jnp.float32)
    ratios = []
    partial_value = [[] for _ in range(fields)]
    ratio_prev = None
    for level in range(levels):
        lower_c = coupling_ref[level - 1 : level, :] if level > 0 else zero_row
        upper_c = coupling_ref[level : level + 1, :] if level < levels - 1 else zero_row
        diagonal = 1.0 + lower_c + upper_c
        pivot = diagonal if level == 0 else diagonal + lower_c * ratio_prev
        for f in range(fields):
            rhs = state_ref[f, level : level + 1, :]
            if level == 0:
                partial_value[f].append(rhs / pivot)
            else:
                partial_value[f].append((rhs + lower_c * partial_value[f][-1]) / pivot)
        ratio_now = -upper_c / pivot if level < levels - 1 else zero_row
        ratios.append(ratio_now)
        ratio_prev = ratio_now
    lowest = []
    for f in range(fields):
        result = partial_value[f][levels - 1]
        for level in range(levels - 2, -1, -1):
            result = partial_value[f][level] - ratios[level] * result
        lowest.append(result)
    out_ref[0:1, :] = jnp.sqrt(lowest[0] * lowest[0] + lowest[1] * lowest[1] + 0.25)
    out_ref[1:2, :] = lowest[2]


def surface_of(atm_state, mixing):
    columns = atm_state.shape[2]
    return pl.pallas_call(
        surface_kernel,
        out_shape=jax.ShapeDtypeStruct((2, columns), jnp.float32),
        compiler_params=pltpu.CompilerParams(vmem_limit_bytes=8 * 1024 * 1024),
    )(atm_state, mixing)


def on_device(
    land_wind,
    land_moist,
    texture,
    land_index,
    erod_map,
    mass_frac,
    blast_table,
    dest_tile,
    regrid_w,
    atm_state,
    dust_mix,
    mixing,
    settle,
):
    high = lax.Precision.HIGHEST
    nblocks, ncells = land_wind.shape
    columns = atm_state.shape[2]
    nbins = blast_table.shape[1]
    devices = lax.axis_size(("sec", "tile"))
    surface = surface_of(atm_state, mixing).astype(jnp.bfloat16).reshape(1, 2 * columns)
    base_thresh = threshold_table(mass_frac.shape[1])
    erodible = lookup(erod_map, land_index)
    emission = emit(land_wind, land_moist, texture, erodible, mass_frac, blast_table, base_thresh)
    partial_flux = jnp.einsum(
        "gkl,gla->gka", emission, regrid_w, preferred_element_type=jnp.float32
    )
    flat_flux = partial_flux.reshape(nblocks, nbins * columns)
    targets = dest_tile[:, 0]
    onehot = (targets[:, None] == jnp.arange(devices)[None, :]).astype(jnp.float32)
    dims = (((0,), (0,)), ((), ()))
    outgoing = lax.dot_general(onehot, flat_flux, dims, precision=high)
    spread = jnp.broadcast_to(surface, (devices, 2 * columns))
    half = nbins * columns // 2
    payload = jnp.concatenate(
        [outgoing.astype(jnp.bfloat16).reshape(devices, 2, half), spread.reshape(devices, 2, columns)], axis=2
    )
    incoming = lax.all_to_all(payload, ("sec", "tile"), split_axis=0, concat_axis=0, tiled=True)
    flux = jnp.sum(incoming[:, :, :half].astype(jnp.float32), axis=0).reshape(nbins, columns)
    gathered = incoming[:, :, half:].reshape(devices, 2 * columns)
    flux = flux * (float(columns) / float(ncells * nblocks))
    loaded = dust_mix.at[:, 0, :].add(flux)
    dust_out = solve(loaded, mixing, settle)
    picked = jnp.dot(onehot.astype(jnp.bfloat16), gathered, preferred_element_type=jnp.float32)
    picked = picked.astype(jnp.bfloat16).reshape(nblocks, 2, columns)
    picked = jnp.concatenate([picked, jnp.ones((nblocks, 1, columns), jnp.bfloat16)], axis=1)
    numer = jnp.einsum("gla,gka->kgl", regrid_w, picked, preferred_element_type=jnp.float32)
    denom = numer[2]
    land_fields = jnp.stack([numer[0] / denom, 0.5 * land_moist + 0.5 * numer[1] / denom])
    return (land_fields, dust_out)


def solution(mesh):
    in_specs = (
        P(("sec", "tile"), None),
        P(("sec", "tile"), None),
        P(("sec", "tile"), None),
        P(("sec", "tile"), None),
        P(("sec", "tile")),
        P(),
        P(),
        P(("sec", "tile"), None),
        P(("sec", "tile"), None, None),
        P(None, None, ("sec", "tile")),
        P(None, None, ("sec", "tile")),
        P(None, ("sec", "tile")),
        P(),
    )
    out_specs = (P(None, ("sec", "tile"), None), P(None, None, ("sec", "tile")))
    return jax.shard_map(
        on_device, mesh=mesh, in_specs=in_specs, out_specs=out_specs, check_vma=False
    )
```

```python
import jax
import jax.numpy as jnp
from jax import lax
from jax.experimental import pallas as pl
from jax.experimental.pallas import tpu as pltpu
from jax.sharding import PartitionSpec as P


def threshold_table(count):
    diameter = 4e-05 * jnp.power(jnp.float32(1.35), jnp.arange(count).astype(jnp.float32))
    return jnp.sqrt(0.0123 * (2160.0 * 9.81 * diameter + 0.0003 / (1.227 * diameter)))


def emit(wind_rows, wind_square, moist_rows, texture_rows, erodible, mass_frac, blast_table, base_thresh):
    high = lax.Precision.HIGHEST
    thresh = base_thresh[:, None, None] * jnp.sqrt(1.0 + 12.1 * moist_rows)[None]
    classes = jnp.arange(mass_frac.shape[0])
    onehot = (texture_rows[None] == classes[:, None, None]).astype(jnp.float32)
    fraction = jnp.einsum("tb,tnl->bnl", mass_frac, onehot, precision=high)
    speed = wind_rows[None]
    salt = (
        40.0
        * fraction
        * erodible[None]
        * (speed + thresh)
        * jnp.maximum(wind_square[None] - thresh * thresh, 0.0)
    )
    blasted = jnp.einsum("tkb,bnl->tknl", blast_table, salt, precision=high)
    emission = jnp.sum(blasted * onehot[:, None], axis=0)
    return jnp.transpose(emission, (1, 0, 2)).astype(jnp.bfloat16)


def lookup_kernel(index_ref, parts_ref, wind_ref, out_ref, square_ref):
    rows_per_step, lanes = index_ref.shape
    segments = parts_ref.shape[1] // 3
    levels = lax.broadcasted_iota(jnp.int32, (segments, lanes), 0).astype(jnp.bfloat16)
    lane_rows = lax.broadcasted_iota(jnp.int32, (128, lanes), 0)
    one = jnp.ones((segments, lanes), jnp.bfloat16)
    zero = jnp.zeros((segments, lanes), jnp.bfloat16)
    square_ref[...] = wind_ref[...] * wind_ref[...]
    for r in range(rows_per_step):
        cell = index_ref[r : r + 1, :]
        high_part = (cell // 128).astype(jnp.bfloat16)
        low_part = cell % 128
        pick_row = jnp.where(levels == high_part, one, zero)
        stacked = jnp.concatenate([pick_row, pick_row, pick_row], axis=0)
        row_values = jnp.dot(parts_ref[...], stacked, preferred_element_type=jnp.float32)
        pick_lane = lane_rows == low_part
        out_ref[r : r + 1, :] = jnp.sum(jnp.where(pick_lane, row_values, 0.0), axis=0, keepdims=True)


def lookup(table, index, wind):
    segments = table.shape[0] // 128
    grid = table.reshape(segments, 128)
    first_wide = lax.reduce_precision(grid, exponent_bits=8, mantissa_bits=7)
    rest = grid - first_wide
    second_wide = lax.reduce_precision(rest, exponent_bits=8, mantissa_bits=7)
    parts = jnp.concatenate([first_wide, second_wide, rest - second_wide], axis=0).T.astype(jnp.bfloat16)
    rows, lanes = index.shape
    step = 128
    return pl.pallas_call(
        lookup_kernel,
        out_shape=(jax.ShapeDtypeStruct((rows, lanes), jnp.float32),) * 2,
        grid=(rows // step,),
        in_specs=[
            pl.BlockSpec((step, lanes), lambda i: (i, 0)),
            pl.BlockSpec((128, 3 * segments), lambda i: (0, 0)),
            pl.BlockSpec((step, lanes), lambda i: (i, 0)),
        ],
        out_specs=(pl.BlockSpec((step, lanes), lambda i: (i, 0)),) * 2,
        compiler_params=pltpu.CompilerParams(vmem_limit_bytes=8 * 1024 * 1024),
        cost_estimate=pl.CostEstimate(
            flops=2 * 384 * segments * rows * lanes, transcendentals=0,
            bytes_accessed=8 * rows * lanes + 768 * segments,
        ),
    )(index, parts, wind)

def solve(right_side, coupling, sinking):
    levels = right_side.shape[1]
    sink_col = sinking[:, None]
    zero_row = jnp.zeros_like(coupling[0])
    ratios = []
    partial_value = []
    ratio_prev = None
    part_prev = None
    for level in range(levels):
        lower_c = coupling[level - 1] if level > 0 else zero_row
        upper_c = coupling[level] if level < levels - 1 else zero_row
        diagonal = 1.0 + lower_c[None] + upper_c[None] + sink_col
        if level == 0:
            pivot = diagonal
            part_now = right_side[:, level] / pivot
        else:
            pivot = diagonal + lower_c[None] * ratio_prev
            part_now = (right_side[:, level] + lower_c[None] * part_prev) / pivot
        if level < levels - 1:
            ratio_now = -(upper_c[None] + sink_col) / pivot
        else:
            ratio_now = jnp.zeros_like(pivot)
        ratios.append(ratio_now)
        partial_value.append(part_now)
        ratio_prev = ratio_now
        part_prev = part_now
    result = [None] * levels
    result[levels - 1] = partial_value[levels - 1]
    for level in range(levels - 2, -1, -1):
        result[level] = partial_value[level] - ratios[level] * result[level + 1]
    return jnp.stack(result, axis=1)


def surface_kernel(state_ref, coupling_ref, out_ref):
    fields, levels, columns = state_ref.shape
    zero_row = jnp.zeros((1, columns), jnp.float32)
    ratios = []
    partial_value = [[] for _ in range(fields)]
    ratio_prev = None
    for level in range(levels):
        lower_c = coupling_ref[level - 1 : level, :] if level > 0 else zero_row
        upper_c = coupling_ref[level : level + 1, :] if level < levels - 1 else zero_row
        diagonal = 1.0 + lower_c + upper_c
        pivot = diagonal if level == 0 else diagonal + lower_c * ratio_prev
        for f in range(fields):
            rhs = state_ref[f, level : level + 1, :]
            if level == 0:
                partial_value[f].append(rhs / pivot)
            else:
                partial_value[f].append((rhs + lower_c * partial_value[f][-1]) / pivot)
        ratio_now = -upper_c / pivot if level < levels - 1 else zero_row
        ratios.append(ratio_now)
        ratio_prev = ratio_now
    lowest = []
    for f in range(fields):
        result = partial_value[f][levels - 1]
        for level in range(levels - 2, -1, -1):
            result = partial_value[f][level] - ratios[level] * result
        lowest.append(result)
    out_ref[0:1, :] = jnp.sqrt(lowest[0] * lowest[0] + lowest[1] * lowest[1] + 0.25)
    out_ref[1:2, :] = lowest[2]


def surface_of(atm_state, mixing):
    columns = atm_state.shape[2]
    return pl.pallas_call(
        surface_kernel,
        out_shape=jax.ShapeDtypeStruct((2, columns), jnp.float32),
        compiler_params=pltpu.CompilerParams(vmem_limit_bytes=8 * 1024 * 1024),
    )(atm_state, mixing)


def on_device(
    land_wind,
    land_moist,
    texture,
    land_index,
    erod_map,
    mass_frac,
    blast_table,
    dest_tile,
    regrid_w,
    atm_state,
    dust_mix,
    mixing,
    settle,
):
    high = lax.Precision.HIGHEST
    nblocks, ncells = land_wind.shape
    columns = atm_state.shape[2]
    nbins = blast_table.shape[1]
    devices = lax.axis_size(("sec", "tile"))
    surface = surface_of(atm_state, mixing).astype(jnp.bfloat16).reshape(1, 2 * columns)
    base_thresh = threshold_table(mass_frac.shape[1])
    erodible, wind_square = lookup(erod_map, land_index, land_wind)
    emission = emit(land_wind, wind_square, land_moist, texture, erodible, mass_frac, blast_table, base_thresh)
    partial_flux = jnp.einsum(
        "gkl,gla->gka", emission, regrid_w, preferred_element_type=jnp.float32
    )
    flat_flux = partial_flux.reshape(nblocks, nbins * columns)
    targets = dest_tile[:, 0]
    onehot = (targets[:, None] == jnp.arange(devices)[None, :]).astype(jnp.float32)
    dims = (((0,), (0,)), ((), ()))
    outgoing = lax.dot_general(onehot, flat_flux, dims, precision=high)
    spread = jnp.broadcast_to(surface, (devices, 2 * columns))
    half = nbins * columns // 2
    payload = jnp.concatenate(
        [outgoing.astype(jnp.bfloat16).reshape(devices, 2, half), spread.reshape(devices, 2, columns)], axis=2
    )
    incoming = lax.all_to_all(payload, ("sec", "tile"), split_axis=0, concat_axis=0, tiled=True)
    flux = jnp.sum(incoming[:, :, :half].astype(jnp.float32), axis=0).reshape(nbins, columns)
    gathered = incoming[:, :, half:].reshape(devices, 2 * columns)
    flux = flux * (float(columns) / float(ncells * nblocks))
    loaded = dust_mix.at[:, 0, :].add(flux)
    dust_out = solve(loaded, mixing, settle)
    picked = jnp.dot(onehot.astype(jnp.bfloat16), gathered, preferred_element_type=jnp.float32)
    picked = picked.astype(jnp.bfloat16).reshape(nblocks, 2, columns)
    picked = jnp.concatenate([picked, jnp.ones((nblocks, 1, columns), jnp.bfloat16)], axis=1)
    numer = jnp.einsum("gla,gka->kgl", regrid_w, picked, preferred_element_type=jnp.float32)
    denom = numer[2]
    land_fields = jnp.stack([numer[0] / denom, 0.5 * land_moist + 0.5 * numer[1] / denom])
    return (land_fields, dust_out)


def solution(mesh):
    in_specs = (
        P(("sec", "tile"), None),
        P(("sec", "tile"), None),
        P(("sec", "tile"), None),
        P(("sec", "tile"), None),
        P(("sec", "tile")),
        P(),
        P(),
        P(("sec", "tile"), None),
        P(("sec", "tile"), None, None),
        P(None, None, ("sec", "tile")),
        P(None, None, ("sec", "tile")),
        P(None, ("sec", "tile")),
        P(),
    )
    out_specs = (P(None, ("sec", "tile"), None), P(None, None, ("sec", "tile")))
    return jax.shard_map(
        on_device, mesh=mesh, in_specs=in_specs, out_specs=out_specs, check_vma=False
    )
```

```python
import jax
import jax.numpy as jnp
from jax import lax
from jax.experimental import pallas as pl
from jax.experimental.pallas import tpu as pltpu
from jax.sharding import PartitionSpec as P


def threshold_table(count):
    diameter = 4e-05 * jnp.power(jnp.float32(1.35), jnp.arange(count).astype(jnp.float32))
    return jnp.sqrt(0.0123 * (2160.0 * 9.81 * diameter + 0.0003 / (1.227 * diameter)))


def emit(wind_rows, wind_square, moist_rows, onehot, erodible, mass_frac, blast_table, base_thresh):
    high = lax.Precision.HIGHEST
    thresh = base_thresh[:, None, None] * jnp.sqrt(1.0 + 12.1 * moist_rows)[None]
    classes = jnp.arange(mass_frac.shape[0])
    fraction = jnp.einsum("tb,tnl->bnl", mass_frac, onehot, precision=high)
    speed = wind_rows[None]
    salt = (
        40.0
        * fraction
        * erodible[None]
        * (speed + thresh)
        * jnp.maximum(wind_square[None] - thresh * thresh, 0.0)
    )
    blasted = jnp.einsum("tkb,bnl->tknl", blast_table, salt, precision=high)
    emission = jnp.sum(blasted * onehot[:, None], axis=0)
    return jnp.transpose(emission, (1, 0, 2)).astype(jnp.bfloat16)


def lookup_kernel(index_ref, parts_ref, wind_ref, texture_ref, out_ref, square_ref, classes_ref):
    rows_per_step, lanes = index_ref.shape
    segments = parts_ref.shape[1] // 3
    levels = lax.broadcasted_iota(jnp.int32, (segments, lanes), 0).astype(jnp.bfloat16)
    lane_rows = lax.broadcasted_iota(jnp.int32, (128, lanes), 0)
    one = jnp.ones((segments, lanes), jnp.bfloat16)
    zero = jnp.zeros((segments, lanes), jnp.bfloat16)
    square_ref[...] = wind_ref[...] * wind_ref[...]
    for t in range(classes_ref.shape[0]):
        classes_ref[t] = jnp.where(texture_ref[...] == t, 1.0, 0.0)
    for r in range(rows_per_step):
        cell = index_ref[r : r + 1, :]
        high_part = (cell // 128).astype(jnp.bfloat16)
        low_part = cell % 128
        pick_row = jnp.where(levels == high_part, one, zero)
        stacked = jnp.concatenate([pick_row, pick_row, pick_row], axis=0)
        row_values = jnp.dot(parts_ref[...], stacked, preferred_element_type=jnp.float32)
        pick_lane = lane_rows == low_part
        out_ref[r : r + 1, :] = jnp.sum(jnp.where(pick_lane, row_values, 0.0), axis=0, keepdims=True)


def lookup(table, index, wind, texture, classes):
    segments = table.shape[0] // 128
    grid = table.reshape(segments, 128)
    first_wide = lax.reduce_precision(grid, exponent_bits=8, mantissa_bits=7)
    rest = grid - first_wide
    second_wide = lax.reduce_precision(rest, exponent_bits=8, mantissa_bits=7)
    parts = jnp.concatenate([first_wide, second_wide, rest - second_wide], axis=0).T.astype(jnp.bfloat16)
    rows, lanes = index.shape
    step = 128
    return pl.pallas_call(
        lookup_kernel,
        out_shape=(jax.ShapeDtypeStruct((rows, lanes), jnp.float32),) * 2
        + (jax.ShapeDtypeStruct((classes, rows, lanes), jnp.float32),),
        grid=(rows // step,),
        in_specs=[
            pl.BlockSpec((step, lanes), lambda i: (i, 0)),
            pl.BlockSpec((128, 3 * segments), lambda i: (0, 0)),
            pl.BlockSpec((step, lanes), lambda i: (i, 0)),
            pl.BlockSpec((step, lanes), lambda i: (i, 0)),
        ],
        out_specs=(pl.BlockSpec((step, lanes), lambda i: (i, 0)),) * 2
        + (pl.BlockSpec((classes, step, lanes), lambda i: (0, i, 0)),),
        compiler_params=pltpu.CompilerParams(vmem_limit_bytes=8 * 1024 * 1024),
        cost_estimate=pl.CostEstimate(
            flops=2 * 384 * segments * rows * lanes, transcendentals=0,
            bytes_accessed=8 * rows * lanes + 768 * segments,
        ),
    )(index, parts, wind, texture)

def solve(right_side, coupling, sinking):
    levels = right_side.shape[1]
    sink_col = sinking[:, None]
    zero_row = jnp.zeros_like(coupling[0])
    ratios = []
    partial_value = []
    ratio_prev = None
    part_prev = None
    for level in range(levels):
        lower_c = coupling[level - 1] if level > 0 else zero_row
        upper_c = coupling[level] if level < levels - 1 else zero_row
        diagonal = 1.0 + lower_c[None] + upper_c[None] + sink_col
        if level == 0:
            pivot = diagonal
            part_now = right_side[:, level] / pivot
        else:
            pivot = diagonal + lower_c[None] * ratio_prev
            part_now = (right_side[:, level] + lower_c[None] * part_prev) / pivot
        if level < levels - 1:
            ratio_now = -(upper_c[None] + sink_col) / pivot
        else:
            ratio_now = jnp.zeros_like(pivot)
        ratios.append(ratio_now)
        partial_value.append(part_now)
        ratio_prev = ratio_now
        part_prev = part_now
    result = [None] * levels
    result[levels - 1] = partial_value[levels - 1]
    for level in range(levels - 2, -1, -1):
        result[level] = partial_value[level] - ratios[level] * result[level + 1]
    return jnp.stack(result, axis=1)


def surface_kernel(state_ref, coupling_ref, out_ref):
    fields, levels, columns = state_ref.shape
    zero_row = jnp.zeros((1, columns), jnp.float32)
    ratios = []
    partial_value = [[] for _ in range(fields)]
    ratio_prev = None
    for level in range(levels):
        lower_c = coupling_ref[level - 1 : level, :] if level > 0 else zero_row
        upper_c = coupling_ref[level : level + 1, :] if level < levels - 1 else zero_row
        diagonal = 1.0 + lower_c + upper_c
        pivot = diagonal if level == 0 else diagonal + lower_c * ratio_prev
        for f in range(fields):
            rhs = state_ref[f, level : level + 1, :]
            if level == 0:
                partial_value[f].append(rhs / pivot)
            else:
                partial_value[f].append((rhs + lower_c * partial_value[f][-1]) / pivot)
        ratio_now = -upper_c / pivot if level < levels - 1 else zero_row
        ratios.append(ratio_now)
        ratio_prev = ratio_now
    lowest = []
    for f in range(fields):
        result = partial_value[f][levels - 1]
        for level in range(levels - 2, -1, -1):
            result = partial_value[f][level] - ratios[level] * result
        lowest.append(result)
    out_ref[0:1, :] = jnp.sqrt(lowest[0] * lowest[0] + lowest[1] * lowest[1] + 0.25)
    out_ref[1:2, :] = lowest[2]


def surface_of(atm_state, mixing):
    columns = atm_state.shape[2]
    return pl.pallas_call(
        surface_kernel,
        out_shape=jax.ShapeDtypeStruct((2, columns), jnp.float32),
        compiler_params=pltpu.CompilerParams(vmem_limit_bytes=8 * 1024 * 1024),
    )(atm_state, mixing)


def on_device(
    land_wind,
    land_moist,
    texture,
    land_index,
    erod_map,
    mass_frac,
    blast_table,
    dest_tile,
    regrid_w,
    atm_state,
    dust_mix,
    mixing,
    settle,
):
    high = lax.Precision.HIGHEST
    nblocks, ncells = land_wind.shape
    columns = atm_state.shape[2]
    nbins = blast_table.shape[1]
    devices = lax.axis_size(("sec", "tile"))
    surface = surface_of(atm_state, mixing).astype(jnp.bfloat16).reshape(1, 2 * columns)
    base_thresh = threshold_table(mass_frac.shape[1])
    erodible, wind_square, texture_onehot = lookup(erod_map, land_index, land_wind, texture, mass_frac.shape[0])
    emission = emit(land_wind, wind_square, land_moist, texture_onehot, erodible, mass_frac, blast_table, base_thresh)
    partial_flux = jnp.einsum(
        "gkl,gla->gka", emission, regrid_w, preferred_element_type=jnp.float32
    )
    flat_flux = partial_flux.reshape(nblocks, nbins * columns)
    targets = dest_tile[:, 0]
    onehot = (targets[:, None] == jnp.arange(devices)[None, :]).astype(jnp.float32)
    dims = (((0,), (0,)), ((), ()))
    outgoing = lax.dot_general(onehot, flat_flux, dims, precision=high)
    spread = jnp.broadcast_to(surface, (devices, 2 * columns))
    half = nbins * columns // 2
    payload = jnp.concatenate(
        [outgoing.astype(jnp.bfloat16).reshape(devices, 2, half), spread.reshape(devices, 2, columns)], axis=2
    )
    incoming = lax.all_to_all(payload, ("sec", "tile"), split_axis=0, concat_axis=0, tiled=True)
    flux = jnp.sum(incoming[:, :, :half].astype(jnp.float32), axis=0).reshape(nbins, columns)
    gathered = incoming[:, :, half:].reshape(devices, 2 * columns)
    flux = flux * (float(columns) / float(ncells * nblocks))
    loaded = dust_mix.at[:, 0, :].add(flux)
    dust_out = solve(loaded, mixing, settle)
    picked = jnp.dot(onehot.astype(jnp.bfloat16), gathered, preferred_element_type=jnp.float32)
    picked = picked.astype(jnp.bfloat16).reshape(nblocks, 2, columns)
    picked = jnp.concatenate([picked, jnp.ones((nblocks, 1, columns), jnp.bfloat16)], axis=1)
    numer = jnp.einsum("gla,gka->kgl", regrid_w, picked, preferred_element_type=jnp.float32)
    denom = numer[2]
    land_fields = jnp.stack([numer[0] / denom, 0.5 * land_moist + 0.5 * numer[1] / denom])
    return (land_fields, dust_out)


def solution(mesh):
    in_specs = (
        P(("sec", "tile"), None),
        P(("sec", "tile"), None),
        P(("sec", "tile"), None),
        P(("sec", "tile"), None),
        P(("sec", "tile")),
        P(),
        P(),
        P(("sec", "tile"), None),
        P(("sec", "tile"), None, None),
        P(None, None, ("sec", "tile")),
        P(None, None, ("sec", "tile")),
        P(None, ("sec", "tile")),
        P(),
    )
    out_specs = (P(None, ("sec", "tile"), None), P(None, None, ("sec", "tile")))
    return jax.shard_map(
        on_device, mesh=mesh, in_specs=in_specs, out_specs=out_specs, check_vma=False
    )
```
